256 devices in a mesh: gx: 32 (over x, y, core), gy: 8 (over z).
Axes of the slice: x: 4, y: 4, z: 8, core: 2. Of those that a mesh axis runs over, the one named last changes fastest.
Arguments:
- orbitals: float32 [64, 128, 64, 128], P(None, 'gx', 'gy'), may hold values from -60 to 60, as said below
- potential: float32 [128, 64, 128], P('gx', 'gy'), may hold values from 0.2 to 2
Outputs:
- basis: float32 [64, 128, 64, 128], P(None, 'gx', 'gy')
- factor: float32 [64, 64], replicated
The draws below stay inside these ranges and needn't reach their ends.
Inputs may be any that keep to these rules, and one draw needn't show every extreme that they name: `orbitals`: Real-valued entries.
All inputs are finite; a program needn't handle non-finite values.
Results may differ from the reference program's by a relative error of at most 0.00011.
Values sent between devices are 32-bit elements; how exact they have to be, the bound alone decides.
No kernel may reach another device: no remote copies, remote signals or barrier semaphores. Data moves between devices by JAX's collectives and lax.ppermute only.
A program may use at most 64 MiB of HBM per device.

```python
import math
import jax
import jax.numpy as jnp
from jax import lax

M = 64
NX = 128
NY = 64
NZ = 128


def draw_orbitals(key, part):
    key_base = jax.random.fold_in(jax.random.fold_in(key, 7), 0)
    spots = jnp.arange(NX, dtype=jnp.float32) / max(NX - 1, 1)
    profile = (1.0 + 2.0 * spots)[None, :, None, None]
    base = jax.random.truncated_normal(key_base, -4.0, 4.0, (M, NX, NY, NZ), jnp.float32)
    return base * profile


def steps_of(rng, extent, pieces, smallest, high):
    factor_of = 1.0
    for position, parts in pieces:
        steps = jax.random.uniform(jax.random.fold_in(jax.random.fold_in(rng, 6), position), (parts,), jnp.float32, smallest / len(pieces), high / len(pieces))
        factor_of = factor_of * jnp.repeat(jnp.exp(steps), extent[position] // parts).reshape((-1,) + (1,) * (len(extent) - 1 - position))
    return factor_of


def setup_inputs(seed: int = 0) -> dict:
    key_list = jax.random.split(jax.random.key(seed), 3)
    return {
        "orbitals": draw_orbitals(jax.random.fold_in(key_list[2], 71), 0),
        "potential": jnp.clip(jnp.exp(math.log(2.0) - 2.3025851 * jax.random.uniform(key_list[1], (NX, NY, NZ), jnp.float32) ** steps_of(key_list[1], (NX, NY, NZ), ((0, 32), (1, 8)), -0.2, 0.2)), 0.2, 2.0),
    }


def laplace_roll(field):
    total = jnp.zeros_like(field)
    for axis_num in range(3):
        total = total - 2.5 * field
        total = total + 4.0 / 3.0 * (jnp.roll(field, 1, axis_num) + jnp.roll(field, -1, axis_num))
        total = total - 1.0 / 12.0 * (jnp.roll(field, 2, axis_num) + jnp.roll(field, -2, axis_num))
    return total

def filter_one(field, potential):
    first = (-0.5 * laplace_roll(field) + potential * field - 5.5 * field) / 4.5
    applied = -0.5 * laplace_roll(first) + potential * first
    return 2.0 * (applied - 5.5 * first) / 4.5 - field

def reference(orbitals, potential):
    filtered = lax.map(lambda one: filter_one(one, potential), orbitals)
    cells = NX * NY * NZ
    flat = filtered.reshape(M, cells)
    gram = jnp.dot(flat.astype(jnp.float32), flat.T.astype(jnp.float32), precision=lax.Precision.HIGHEST, preferred_element_type=jnp.float32) / cells
    factor = lax.linalg.cholesky(gram).T
    solved = lax.linalg.triangular_solve(factor, flat, left_side=True, lower=False, transpose_a=True)
    basis = (solved * jnp.sqrt(jnp.float32(cells))).reshape(M, NX, NY, NZ)
    return (basis, factor)
```

```python
import jax
import jax.numpy as jnp
from jax import lax
from jax.experimental import pallas as pl
from jax.experimental.pallas import tpu as pltpu
from jax.sharding import PartitionSpec as P


def extended(cells, sides, width):
    for axis, dim in sides:
        count = lax.axis_size(axis)
        head = lax.slice_in_dim(cells, 0, width, axis=dim)
        tail = lax.slice_in_dim(cells, cells.shape[dim] - width, cells.shape[dim], axis=dim)
        cells = jnp.concatenate(
            [
                lax.ppermute(tail, axis, [(i, (i + 1) % count) for i in range(count)]),
                cells,
                lax.ppermute(head, axis, [((i + 1) % count, i) for i in range(count)]),
            ],
            axis=dim,
        )
    return cells


def apply_ham(padded, pot):
    core = padded[:, 2:-2, 2:-2]
    total = -7.5 * core
    total = total + 4.0 / 3.0 * (padded[:, 3:-1, 2:-2] + padded[:, 1:-3, 2:-2])
    total = total - 1.0 / 12.0 * (padded[:, 4:, 2:-2] + padded[:, :-4, 2:-2])
    total = total + 4.0 / 3.0 * (padded[:, 2:-2, 3:-1] + padded[:, 2:-2, 1:-3])
    total = total - 1.0 / 12.0 * (padded[:, 2:-2, 4:] + padded[:, 2:-2, :-4])
    total = total + 4.0 / 3.0 * (jnp.roll(core, 1, 3) + jnp.roll(core, -1, 3))
    total = total - 1.0 / 12.0 * (jnp.roll(core, 2, 3) + jnp.roll(core, -2, 3))
    return -0.5 * total + pot[None] * core


def with_faces(field):
    return extended(field, (("gx", 1), ("gy", 2)), 2)


def factor_kernel(aug_ref, out_ref):
    order = aug_ref.shape[0]
    groups = order // 8
    blocks = [aug_ref[pl.ds(8 * i, 8), :] for i in range(groups)]
    sub = lax.broadcasted_iota(jnp.int32, blocks[0].shape, 0)
    lane = lax.broadcasted_iota(jnp.int32, blocks[0].shape, 1)
    for k in range(order):
        home, place = divmod(k, 8)
        row = jnp.sum(jnp.where(sub == place, blocks[home], 0.0), axis=0, keepdims=True)
        pivot = jnp.sum(jnp.where(lane[:1] == k, row, 0.0), axis=1, keepdims=True)
        scale = 1.0 / jnp.sqrt(pivot)
        scaled = row * scale
        for j in range(home, groups):
            block = blocks[j]
            column = jnp.sum(jnp.where(lane == k, block, 0.0), axis=1, keepdims=True) * scale
            if j == home:
                column = jnp.where(sub[:, :1] > place, column, 0.0)
                block = jnp.where(sub == place, scaled, block - column * scaled)
            else:
                block = block - column * scaled
            blocks[j] = block
    for i in range(groups):
        keep = (lane >= order) | (lane >= sub + 8 * i)
        out_ref[pl.ds(8 * i, 8), :] = jnp.where(keep, blocks[i], 0.0)


def factor_and_inverse(gram):
    order = gram.shape[0]
    sym = 0.5 * (gram + gram.T)
    aug = jnp.concatenate([sym, jnp.eye(order, dtype=jnp.float32)], axis=1)
    out = pl.pallas_call(
        factor_kernel,
        out_shape=jax.ShapeDtypeStruct(aug.shape, jnp.float32),
        in_specs=[pl.BlockSpec(memory_space=pltpu.VMEM)],
        out_specs=pl.BlockSpec(memory_space=pltpu.VMEM),
    )(aug)
    return out[:, :order], out[:, order:]


def shards(orbitals, potential):
    first = (apply_ham(with_faces(orbitals), potential) - 5.5 * orbitals) / 4.5
    applied = apply_ham(with_faces(first), potential)
    filtered = 2.0 * (applied - 5.5 * first) / 4.5 - orbitals
    width = filtered.shape[0]
    flat = filtered.reshape(width, -1)
    cells = flat.shape[1] * lax.axis_size("gx") * lax.axis_size("gy")
    local_gram = (
        jnp.dot(flat, flat.T, precision=lax.Precision.HIGHEST, preferred_element_type=jnp.float32)
        / cells
    )
    factor, lower_inverse = factor_and_inverse(lax.psum(local_gram, ("gx", "gy")))
    solved = jnp.dot(
        lower_inverse, flat, precision=lax.Precision.HIGHEST, preferred_element_type=jnp.float32
    )
    basis = (solved * jnp.sqrt(jnp.float32(cells))).reshape(filtered.shape)
    return (basis, factor)


def solution(mesh):
    return jax.shard_map(
        shards,
        mesh=mesh,
        in_specs=(P(None, "gx", "gy", None), P("gx", "gy", None)),
        out_specs=(P(None, "gx", "gy", None), P()),
        check_vma=False,
    )
```

```python
import jax
import jax.numpy as jnp
from jax import lax
from jax.experimental import pallas as pl
from jax.experimental.pallas import tpu as pltpu
from jax.sharding import PartitionSpec as P


def extended(cells, sides, width):
    for axis, dim in sides:
        count = lax.axis_size(axis)
        head = lax.slice_in_dim(cells, 0, width, axis=dim)
        tail = lax.slice_in_dim(cells, cells.shape[dim] - width, cells.shape[dim], axis=dim)
        cells = jnp.concatenate(
            [
                lax.ppermute(tail, axis, [(i, (i + 1) % count) for i in range(count)]),
                cells,
                lax.ppermute(head, axis, [((i + 1) % count, i) for i in range(count)]),
            ],
            axis=dim,
        )
    return cells


def apply_ham(padded, pot):
    core = padded[:, 2:-2, 2:-2]
    total = -7.5 * core
    total = total + 4.0 / 3.0 * (padded[:, 3:-1, 2:-2] + padded[:, 1:-3, 2:-2])
    total = total - 1.0 / 12.0 * (padded[:, 4:, 2:-2] + padded[:, :-4, 2:-2])
    total = total + 4.0 / 3.0 * (padded[:, 2:-2, 3:-1] + padded[:, 2:-2, 1:-3])
    total = total - 1.0 / 12.0 * (padded[:, 2:-2, 4:] + padded[:, 2:-2, :-4])
    total = total + 4.0 / 3.0 * (jnp.roll(core, 1, 3) + jnp.roll(core, -1, 3))
    total = total - 1.0 / 12.0 * (jnp.roll(core, 2, 3) + jnp.roll(core, -2, 3))
    return -0.5 * total + pot[None] * core


def with_faces(field):
    return extended(field, (("gx", 1), ("gy", 2)), 2)


def factor_kernel(aug_ref, out_ref):
    order = aug_ref.shape[0]
    groups = order // 8
    blocks = [aug_ref[pl.ds(8 * i, 8), :] for i in range(groups)]
    sub = lax.broadcasted_iota(jnp.int32, blocks[0].shape, 0)
    lane = lax.broadcasted_iota(jnp.int32, blocks[0].shape, 1)
    for k in range(order):
        home, place = divmod(k, 8)
        row = jnp.sum(jnp.where(sub == place, blocks[home], 0.0), axis=0, keepdims=True)
        pivot = jnp.sum(jnp.where(lane[:1] == k, row, 0.0), axis=1, keepdims=True)
        scale = 1.0 / jnp.sqrt(pivot)
        scaled = row * scale
        for j in range(home, groups):
            block = blocks[j]
            column = jnp.sum(jnp.where(lane == k, block, 0.0), axis=1, keepdims=True) * scale
            if j == home:
                column = jnp.where(sub[:, :1] > place, column, 0.0)
                block = jnp.where(sub == place, scaled, block - column * scaled)
            else:
                block = block - column * scaled
            blocks[j] = block
    for i in range(groups):
        keep = (lane >= order) | (lane >= sub + 8 * i)
        out_ref[pl.ds(8 * i, 8), :] = jnp.where(keep, blocks[i], 0.0)


def factor_and_inverse(gram):
    order = gram.shape[0]
    sym = 0.5 * (gram + gram.T)
    aug = jnp.concatenate([sym, jnp.eye(order, dtype=jnp.float32)], axis=1)
    out = pl.pallas_call(
        factor_kernel,
        out_shape=jax.ShapeDtypeStruct(aug.shape, jnp.float32),
        in_specs=[pl.BlockSpec(memory_space=pltpu.VMEM)],
        out_specs=pl.BlockSpec(memory_space=pltpu.VMEM),
    )(aug)
    return out[:, :order], out[:, order:]


def butterfly_sum(value, axis):
    count = lax.axis_size(axis)
    if count & (count - 1):
        return lax.psum(value, axis)
    mask = 1
    while mask < count:
        value = value + lax.ppermute(value, axis, [(i, i ^ mask) for i in range(count)])
        mask *= 2
    return value


def shards(orbitals, potential):
    first = (apply_ham(with_faces(orbitals), potential) - 5.5 * orbitals) / 4.5
    applied = apply_ham(with_faces(first), potential)
    filtered = 2.0 * (applied - 5.5 * first) / 4.5 - orbitals
    width = filtered.shape[0]
    flat = filtered.reshape(width, -1)
    cells = flat.shape[1] * lax.axis_size("gx") * lax.axis_size("gy")
    local_gram = (
        jnp.dot(flat, flat.T, precision=lax.Precision.HIGHEST, preferred_element_type=jnp.float32)
        / cells
    )
    packed = local_gram.reshape(-1, 128)
    gram = butterfly_sum(butterfly_sum(packed, "gy"), "gx").reshape(local_gram.shape)
    factor, lower_inverse = factor_and_inverse(gram)
    solved = jnp.dot(
        lower_inverse, flat, precision=lax.Precision.HIGHEST, preferred_element_type=jnp.float32
    )
    basis = (solved * jnp.sqrt(jnp.float32(cells))).reshape(filtered.shape)
    return (basis, factor)


def solution(mesh):
    return jax.shard_map(
        shards,
        mesh=mesh,
        in_specs=(P(None, "gx", "gy", None), P("gx", "gy", None)),
        out_specs=(P(None, "gx", "gy", None), P()),
        check_vma=False,
    )
```

```python
import jax
import jax.numpy as jnp
from jax import lax
from jax.experimental import pallas as pl
from jax.experimental.pallas import tpu as pltpu
from jax.sharding import PartitionSpec as P


def faces(cells, axis, dim, width):
    count = lax.axis_size(axis)
    size = cells.shape[dim]
    head = lax.slice_in_dim(cells, 0, width, axis=dim)
    tail = lax.slice_in_dim(cells, size - width, size, axis=dim)
    before = lax.ppermute(tail, axis, [(i, (i + 1) % count) for i in range(count)])
    after = lax.ppermute(head, axis, [((i + 1) % count, i) for i in range(count)])
    return jnp.concatenate([before, cells, after], axis=dim)


def apply_ham(core, pot):
    along_x = faces(core, "gx", 1, 2)
    along_y = faces(core, "gy", 2, 2)
    total = -7.5 * core
    total = total + 4.0 / 3.0 * (along_x[:, 3:-1] + along_x[:, 1:-3])
    total = total - 1.0 / 12.0 * (along_x[:, 4:] + along_x[:, :-4])
    total = total + 4.0 / 3.0 * (along_y[:, :, 3:-1] + along_y[:, :, 1:-3])
    total = total - 1.0 / 12.0 * (along_y[:, :, 4:] + along_y[:, :, :-4])
    total = total + 4.0 / 3.0 * (jnp.roll(core, 1, 3) + jnp.roll(core, -1, 3))
    total = total - 1.0 / 12.0 * (jnp.roll(core, 2, 3) + jnp.roll(core, -2, 3))
    return -0.5 * total + pot[None] * core


def factor_kernel(aug_ref, out_ref):
    order = aug_ref.shape[0]
    groups = order // 8
    blocks = [aug_ref[pl.ds(8 * i, 8), :] for i in range(groups)]
    sub = lax.broadcasted_iota(jnp.int32, blocks[0].shape, 0)
    lane = lax.broadcasted_iota(jnp.int32, blocks[0].shape, 1)
    for k in range(order):
        home, place = divmod(k, 8)
        row = jnp.sum(jnp.where(sub == place, blocks[home], 0.0), axis=0, keepdims=True)
        pivot = jnp.sum(jnp.where(lane[:1] == k, row, 0.0), axis=1, keepdims=True)
        scale = 1.0 / jnp.sqrt(pivot)
        scaled = row * scale
        for j in range(home, groups):
            block = blocks[j]
            column = jnp.sum(jnp.where(lane == k, block, 0.0), axis=1, keepdims=True) * scale
            if j == home:
                column = jnp.where(sub[:, :1] > place, column, 0.0)
                block = jnp.where(sub == place, scaled, block - column * scaled)
            else:
                block = block - column * scaled
            blocks[j] = block
    for i in range(groups):
        keep = (lane >= order) | (lane >= sub + 8 * i)
        out_ref[pl.ds(8 * i, 8), :] = jnp.where(keep, blocks[i], 0.0)


def factor_and_inverse(gram):
    order = gram.shape[0]
    sym = 0.5 * (gram + gram.T)
    aug = jnp.concatenate([sym, jnp.eye(order, dtype=jnp.float32)], axis=1)
    out = pl.pallas_call(
        factor_kernel,
        out_shape=jax.ShapeDtypeStruct(aug.shape, jnp.float32),
        in_specs=[pl.BlockSpec(memory_space=pltpu.VMEM)],
        out_specs=pl.BlockSpec(memory_space=pltpu.VMEM),
    )(aug)
    return out[:, :order], out[:, order:]


def butterfly_sum(value, axis):
    count = lax.axis_size(axis)
    if count & (count - 1):
        return lax.psum(value, axis)
    mask = 1
    while mask < count:
        value = value + lax.ppermute(value, axis, [(i, i ^ mask) for i in range(count)])
        mask *= 2
    return value


def shards(orbitals, potential):
    first = (apply_ham(orbitals, potential) - 5.5 * orbitals) / 4.5
    applied = apply_ham(first, potential)
    filtered = 2.0 * (applied - 5.5 * first) / 4.5 - orbitals
    width = filtered.shape[0]
    flat = filtered.reshape(width, -1)
    cells = flat.shape[1] * lax.axis_size("gx") * lax.axis_size("gy")
    local_gram = (
        jnp.dot(flat, flat.T, precision=lax.Precision.HIGHEST, preferred_element_type=jnp.float32)
        / cells
    )
    packed = local_gram.reshape(-1, 128)
    gram = butterfly_sum(butterfly_sum(packed, "gy"), "gx").reshape(local_gram.shape)
    factor, lower_inverse = factor_and_inverse(gram)
    solved = jnp.dot(
        lower_inverse, flat, precision=lax.Precision.HIGHEST, preferred_element_type=jnp.float32
    )
    basis = (solved * jnp.sqrt(jnp.float32(cells))).reshape(filtered.shape)
    return (basis, factor)


def solution(mesh):
    return jax.shard_map(
        shards,
        mesh=mesh,
        in_specs=(P(None, "gx", "gy", None), P("gx", "gy", None)),
        out_specs=(P(None, "gx", "gy", None), P()),
        check_vma=False,
    )
```

```python
import jax
import jax.numpy as jnp
from jax import lax
from jax.experimental import pallas as pl
from jax.experimental.pallas import tpu as pltpu
from jax.sharding import PartitionSpec as P


def faces(cells, axis, dim, width):
    count = lax.axis_size(axis)
    size = cells.shape[dim]
    head = lax.slice_in_dim(cells, 0, width, axis=dim)
    tail = lax.slice_in_dim(cells, size - width, size, axis=dim)
    before = lax.ppermute(tail, axis, [(i, (i + 1) % count) for i in range(count)])
    after = lax.ppermute(head, axis, [((i + 1) % count, i) for i in range(count)])
    return jnp.concatenate([before, cells, after], axis=dim)


def apply_ham(core, pot):
    along_x = faces(core, "gx", 1, 2)
    along_y = faces(core, "gy", 2, 2)
    total = -7.5 * core
    total = total + 4.0 / 3.0 * (along_x[:, 3:-1] + along_x[:, 1:-3])
    total = total - 1.0 / 12.0 * (along_x[:, 4:] + along_x[:, :-4])
    total = total + 4.0 / 3.0 * (along_y[:, :, 3:-1] + along_y[:, :, 1:-3])
    total = total - 1.0 / 12.0 * (along_y[:, :, 4:] + along_y[:, :, :-4])
    total = total + 4.0 / 3.0 * (jnp.roll(core, 1, 3) + jnp.roll(core, -1, 3))
    total = total - 1.0 / 12.0 * (jnp.roll(core, 2, 3) + jnp.roll(core, -2, 3))
    return -0.5 * total + pot[None] * core


def factor_kernel(aug_ref, out_ref):
    order = aug_ref.shape[0]
    groups = order // 8
    blocks = [aug_ref[pl.ds(8 * i, 8), :] for i in range(groups)]
    sub = lax.broadcasted_iota(jnp.int32, blocks[0].shape, 0)
    lane = lax.broadcasted_iota(jnp.int32, blocks[0].shape, 1)
    for k in range(order):
        home, place = divmod(k, 8)
        row = blocks[home][place:place + 1, :]
        scale = 1.0 / jnp.sqrt(row[:, k:k + 1])
        scaled = row * scale
        for j in range(home, groups):
            block = blocks[j]
            column = block[:, k:k + 1] * scale
            if j == home:
                column = jnp.where(sub[:, :1] > place, column, 0.0)
                block = jnp.where(sub == place, scaled, block - column * scaled)
            else:
                block = block - column * scaled
            blocks[j] = block
    for i in range(groups):
        keep = (lane >= order) | (lane >= sub + 8 * i)
        out_ref[pl.ds(8 * i, 8), :] = jnp.where(keep, blocks[i], 0.0)


def factor_and_inverse(gram):
    order = gram.shape[0]
    sym = 0.5 * (gram + gram.T)
    aug = jnp.concatenate([sym, jnp.eye(order, dtype=jnp.float32)], axis=1)
    out = pl.pallas_call(
        factor_kernel,
        out_shape=jax.ShapeDtypeStruct(aug.shape, jnp.float32),
        in_specs=[pl.BlockSpec(memory_space=pltpu.VMEM)],
        out_specs=pl.BlockSpec(memory_space=pltpu.VMEM),
    )(aug)
    return out[:, :order], out[:, order:]


def butterfly_sum(value, axis):
    count = lax.axis_size(axis)
    if count & (count - 1):
        return lax.psum(value, axis)
    mask = 1
    while mask < count:
        value = value + lax.ppermute(value, axis, [(i, i ^ mask) for i in range(count)])
        mask *= 2
    return value


def shards(orbitals, potential):
    first = (apply_ham(orbitals, potential) - 5.5 * orbitals) / 4.5
    applied = apply_ham(first, potential)
    filtered = 2.0 * (applied - 5.5 * first) / 4.5 - orbitals
    count = filtered.shape[1] * filtered.shape[2] * filtered.shape[3]
    cells = count * lax.axis_size("gx") * lax.axis_size("gy")
    local_gram = (
        jnp.einsum(
            "kxyz,mxyz->km", filtered, filtered,
            precision=lax.Precision.HIGHEST, preferred_element_type=jnp.float32,
        )
        / cells
    )
    packed = local_gram.reshape(-1, 128)
    gram = butterfly_sum(butterfly_sum(packed, "gy"), "gx").reshape(local_gram.shape)
    factor, lower_inverse = factor_and_inverse(gram)
    basis = jnp.einsum(
        "mk,kxyz->mxyz", lower_inverse * jnp.sqrt(jnp.float32(cells)), filtered,
        precision=lax.Precision.HIGHEST, preferred_element_type=jnp.float32,
    )
    return (basis, factor)


def solution(mesh):
    return jax.shard_map(
        shards,
        mesh=mesh,
        in_specs=(P(None, "gx", "gy", None), P("gx", "gy", None)),
        out_specs=(P(None, "gx", "gy", None), P()),
        check_vma=False,
    )
```

```python
import jax
import jax.numpy as jnp
from jax import lax
from jax.experimental import pallas as pl
from jax.experimental.pallas import tpu as pltpu
from jax.sharding import PartitionSpec as P


def faces(cells, axis, dim, width):
    count = lax.axis_size(axis)
    size = cells.shape[dim]
    head = lax.slice_in_dim(cells, 0, width, axis=dim)
    tail = lax.slice_in_dim(cells, size - width, size, axis=dim)
    before = lax.ppermute(tail, axis, [(i, (i + 1) % count) for i in range(count)])
    after = lax.ppermute(head, axis, [((i + 1) % count, i) for i in range(count)])
    return jnp.concatenate([before, cells, after], axis=dim)


def apply_ham(core, pot):
    along_x = faces(core, "gx", 1, 2)
    along_y = faces(core, "gy", 2, 2)
    total = -7.5 * core
    total = total + 4.0 / 3.0 * (along_x[:, 3:-1] + along_x[:, 1:-3])
    total = total - 1.0 / 12.0 * (along_x[:, 4:] + along_x[:, :-4])
    total = total + 4.0 / 3.0 * (along_y[:, :, 3:-1] + along_y[:, :, 1:-3])
    total = total - 1.0 / 12.0 * (along_y[:, :, 4:] + along_y[:, :, :-4])
    total = total + 4.0 / 3.0 * (jnp.roll(core, 1, 3) + jnp.roll(core, -1, 3))
    total = total - 1.0 / 12.0 * (jnp.roll(core, 2, 3) + jnp.roll(core, -2, 3))
    return -0.5 * total + pot[None] * core


def factor_kernel(aug_ref, out_ref):
    order = aug_ref.shape[0]
    groups = order // 8
    blocks = [aug_ref[pl.ds(8 * i, 8), :] for i in range(groups)]
    sub = lax.broadcasted_iota(jnp.int32, blocks[0].shape, 0)
    lane = lax.broadcasted_iota(jnp.int32, blocks[0].shape, 1)
    for k in range(order):
        home, place = divmod(k, 8)
        row = blocks[home][place:place + 1, :]
        scale = 1.0 / jnp.sqrt(row[:, k:k + 1])
        scaled = row * scale
        for j in range(home, groups):
            block = blocks[j]
            column = block[:, k:k + 1] * scale
            if j == home:
                column = jnp.where(sub[:, :1] > place, column, 0.0)
                block = jnp.where(sub == place, scaled, block - column * scaled)
            else:
                block = block - column * scaled
            blocks[j] = block
    for i in range(groups):
        keep = (lane >= order) | (lane >= sub + 8 * i)
        out_ref[pl.ds(8 * i, 8), :] = jnp.where(keep, blocks[i], 0.0)


def factor_and_inverse(gram):
    order = gram.shape[0]
    sym = 0.5 * (gram + gram.T)
    aug = jnp.concatenate([sym, jnp.eye(order, dtype=jnp.float32)], axis=1)
    out = pl.pallas_call(
        factor_kernel,
        out_shape=jax.ShapeDtypeStruct(aug.shape, jnp.float32),
        in_specs=[pl.BlockSpec(memory_space=pltpu.VMEM)],
        out_specs=pl.BlockSpec(memory_space=pltpu.VMEM),
    )(aug)
    return out[:, :order], out[:, order:]


def ring_rounds(stride):
    def flip(i):
        return i ^ stride

    def mirror(i):
        return i + (3 - 2 * ((i // stride) % 4)) * stride

    return [flip, mirror]


def butterfly_sum(value, axis):
    count = lax.axis_size(axis)
    if count & (count - 1):
        return lax.psum(value, axis)
    if count == 32:
        rounds = [lambda i: i ^ 1] + ring_rounds(2) + ring_rounds(8)
    else:
        rounds = [lambda i, mask=1 << b: i ^ mask for b in range(count.bit_length() - 1)]
    for partner in rounds:
        value = value + lax.ppermute(value, axis, [(i, partner(i)) for i in range(count)])
    return value


def shards(orbitals, potential):
    first = (apply_ham(orbitals, potential) - 5.5 * orbitals) / 4.5
    applied = apply_ham(first, potential)
    filtered = 2.0 * (applied - 5.5 * first) / 4.5 - orbitals
    count = filtered.shape[1] * filtered.shape[2] * filtered.shape[3]
    cells = count * lax.axis_size("gx") * lax.axis_size("gy")
    local_gram = (
        jnp.einsum(
            "kxyz,mxyz->km", filtered, filtered,
            precision=lax.Precision.HIGHEST, preferred_element_type=jnp.float32,
        )
        / cells
    )
    packed = local_gram.reshape(-1, 128)
    gram = butterfly_sum(butterfly_sum(packed, "gy"), "gx").reshape(local_gram.shape)
    factor, lower_inverse = factor_and_inverse(gram)
    basis = jnp.einsum(
        "mk,kxyz->mxyz", lower_inverse * jnp.sqrt(jnp.float32(cells)), filtered,
        precision=lax.Precision.HIGHEST, preferred_element_type=jnp.float32,
    )
    return (basis, factor)


def solution(mesh):
    return jax.shard_map(
        shards,
        mesh=mesh,
        in_specs=(P(None, "gx", "gy", None), P("gx", "gy", None)),
        out_specs=(P(None, "gx", "gy", None), P()),
        check_vma=False,
    )
```

```python
import jax
import jax.numpy as jnp
from jax import lax
from jax.experimental import pallas as pl
from jax.experimental.pallas import tpu as pltpu
from jax.sharding import PartitionSpec as P


def faces(cells, axis, dim, width):
    count = lax.axis_size(axis)
    size = cells.shape[dim]
    head = lax.slice_in_dim(cells, 0, width, axis=dim)
    tail = lax.slice_in_dim(cells, size - width, size, axis=dim)
    before = lax.ppermute(tail, axis, [(i, (i + 1) % count) for i in range(count)])
    after = lax.ppermute(head, axis, [((i + 1) % count, i) for i in range(count)])
    return jnp.concatenate([before, cells, after], axis=dim)


def apply_ham(core, pot):
    along_x = faces(core, "gx", 1, 2)
    along_y = faces(core, "gy", 2, 2)
    total = -7.5 * core
    total = total + 4.0 / 3.0 * (along_x[:, 3:-1] + along_x[:, 1:-3])
    total = total - 1.0 / 12.0 * (along_x[:, 4:] + along_x[:, :-4])
    total = total + 4.0 / 3.0 * (along_y[:, :, 3:-1] + along_y[:, :, 1:-3])
    total = total - 1.0 / 12.0 * (along_y[:, :, 4:] + along_y[:, :, :-4])
    total = total + 4.0 / 3.0 * (jnp.roll(core, 1, 3) + jnp.roll(core, -1, 3))
    total = total - 1.0 / 12.0 * (jnp.roll(core, 2, 3) + jnp.roll(core, -2, 3))
    return -0.5 * total + pot[None] * core


def factor_kernel(aug_ref, out_ref):
    order = aug_ref.shape[0]
    groups = order // 8
    blocks = [aug_ref[pl.ds(8 * i, 8), :] for i in range(groups)]
    sub = lax.broadcasted_iota(jnp.int32, blocks[0].shape, 0)
    lane = lax.broadcasted_iota(jnp.int32, blocks[0].shape, 1)
    for k in range(order):
        home, place = divmod(k, 8)
        row = blocks[home][place:place + 1, :]
        inverse = 1.0 / row[:, k:k + 1]
        for j in range(home, groups):
            block = blocks[j]
            column = block[:, k:k + 1] * inverse
            if j == home:
                column = jnp.where(sub[:, :1] > place, column, 0.0)
            blocks[j] = block - column * row
    for i in range(groups):
        block = blocks[i]
        pivots = jnp.sum(jnp.where(lane == sub + 8 * i, block, 0.0), axis=1, keepdims=True)
        keep = (lane >= order) | (lane >= sub + 8 * i)
        out_ref[pl.ds(8 * i, 8), :] = jnp.where(keep, block / jnp.sqrt(pivots), 0.0)


def factor_and_inverse(gram):
    order = gram.shape[0]
    sym = 0.5 * (gram + gram.T)
    aug = jnp.concatenate([sym, jnp.eye(order, dtype=jnp.float32)], axis=1)
    out = pl.pallas_call(
        factor_kernel,
        out_shape=jax.ShapeDtypeStruct(aug.shape, jnp.float32),
        in_specs=[pl.BlockSpec(memory_space=pltpu.VMEM)],
        out_specs=pl.BlockSpec(memory_space=pltpu.VMEM),
    )(aug)
    return out[:, :order], out[:, order:]


def ring_rounds(stride):
    def flip(i):
        return i ^ stride

    def mirror(i):
        return i + (3 - 2 * ((i // stride) % 4)) * stride

    return [flip, mirror]


def butterfly_sum(value, axis):
    count = lax.axis_size(axis)
    if count & (count - 1):
        return lax.psum(value, axis)
    if count == 32:
        rounds = [lambda i: i ^ 1] + ring_rounds(2) + ring_rounds(8)
    else:
        rounds = [lambda i, mask=1 << b: i ^ mask for b in range(count.bit_length() - 1)]
    for partner in rounds:
        value = value + lax.ppermute(value, axis, [(i, partner(i)) for i in range(count)])
    return value


def shards(orbitals, potential):
    first = (apply_ham(orbitals, potential) - 5.5 * orbitals) / 4.5
    applied = apply_ham(first, potential)
    filtered = 2.0 * (applied - 5.5 * first) / 4.5 - orbitals
    count = filtered.shape[1] * filtered.shape[2] * filtered.shape[3]
    cells = count * lax.axis_size("gx") * lax.axis_size("gy")
    local_gram = (
        jnp.einsum(
            "kxyz,mxyz->km", filtered, filtered,
            precision=lax.Precision.HIGHEST, preferred_element_type=jnp.float32,
        )
        / cells
    )
    packed = local_gram.reshape(-1, 128)
    gram = butterfly_sum(butterfly_sum(packed, "gy"), "gx").reshape(local_gram.shape)
    factor, lower_inverse = factor_and_inverse(gram)
    basis = jnp.einsum(
        "mk,kxyz->mxyz", lower_inverse * jnp.sqrt(jnp.float32(cells)), filtered,
        precision=lax.Precision.HIGHEST, preferred_element_type=jnp.float32,
    )
    return (basis, factor)


def solution(mesh):
    return jax.shard_map(
        shards,
        mesh=mesh,
        in_specs=(P(None, "gx", "gy", None), P("gx", "gy", None)),
        out_specs=(P(None, "gx", "gy", None), P()),
        check_vma=False,
    )
```

```python
import jax
import jax.numpy as jnp
from jax import lax
from jax.experimental import pallas as pl
from jax.experimental.pallas import tpu as pltpu
from jax.sharding import PartitionSpec as P


def faces(cells, axis, dim, width):
    count = lax.axis_size(axis)
    size = cells.shape[dim]
    head = lax.slice_in_dim(cells, 0, width, axis=dim)
    tail = lax.slice_in_dim(cells, size - width, size, axis=dim)
    before = lax.ppermute(tail, axis, [(i, (i + 1) % count) for i in range(count)])
    after = lax.ppermute(head, axis, [((i + 1) % count, i) for i in range(count)])
    return jnp.concatenate([before, cells, after], axis=dim)


def apply_ham(core, pot):
    along_x = faces(core, "gx", 1, 2)
    along_y = faces(core, "gy", 2, 2)
    total = -7.5 * core
    total = total + 4.0 / 3.0 * (along_x[:, 3:-1] + along_x[:, 1:-3])
    total = total - 1.0 / 12.0 * (along_x[:, 4:] + along_x[:, :-4])
    total = total + 4.0 / 3.0 * (along_y[:, :, 3:-1] + along_y[:, :, 1:-3])
    total = total - 1.0 / 12.0 * (along_y[:, :, 4:] + along_y[:, :, :-4])
    size = core.shape[3]
    along_z = jnp.concatenate([core[..., size - 2:], core, core[..., :2]], axis=3)
    total = total + 4.0 / 3.0 * (along_z[..., 1:size + 1] + along_z[..., 3:size + 3])
    total = total - 1.0 / 12.0 * (along_z[..., :size] + along_z[..., 4:])
    return -0.5 * total + pot[None] * core


def factor_kernel(aug_ref, out_ref):
    order = aug_ref.shape[0]
    groups = order // 8
    blocks = [aug_ref[pl.ds(8 * i, 8), :] for i in range(groups)]
    sub = lax.broadcasted_iota(jnp.int32, blocks[0].shape, 0)
    lane = lax.broadcasted_iota(jnp.int32, blocks[0].shape, 1)
    for k in range(order):
        home, place = divmod(k, 8)
        row = blocks[home][place:place + 1, :]
        inverse = 1.0 / row[:, k:k + 1]
        for j in range(home, groups):
            block = blocks[j]
            column = block[:, k:k + 1] * inverse
            if j == home:
                column = jnp.where(sub[:, :1] > place, column, 0.0)
            blocks[j] = block - column * row
    for i in range(groups):
        block = blocks[i]
        pivots = jnp.sum(jnp.where(lane == sub + 8 * i, block, 0.0), axis=1, keepdims=True)
        keep = (lane >= order) | (lane >= sub + 8 * i)
        out_ref[pl.ds(8 * i, 8), :] = jnp.where(keep, block / jnp.sqrt(pivots), 0.0)


def factor_and_inverse(gram):
    order = gram.shape[0]
    sym = 0.5 * (gram + gram.T)
    aug = jnp.concatenate([sym, jnp.eye(order, dtype=jnp.float32)], axis=1)
    out = pl.pallas_call(
        factor_kernel,
        out_shape=jax.ShapeDtypeStruct(aug.shape, jnp.float32),
        in_specs=[pl.BlockSpec(memory_space=pltpu.VMEM)],
        out_specs=pl.BlockSpec(memory_space=pltpu.VMEM),
    )(aug)
    return out[:, :order], out[:, order:]


def ring_rounds(stride):
    def flip(i):
        return i ^ stride

    def mirror(i):
        return i + (3 - 2 * ((i // stride) % 4)) * stride

    return [flip, mirror]


def butterfly_sum(value, axis):
    count = lax.axis_size(axis)
    if count & (count - 1):
        return lax.psum(value, axis)
    if count == 32:
        rounds = [lambda i: i ^ 1] + ring_rounds(2) + ring_rounds(8)
    else:
        rounds = [lambda i, mask=1 << b: i ^ mask for b in range(count.bit_length() - 1)]
    for partner in rounds:
        value = value + lax.ppermute(value, axis, [(i, partner(i)) for i in range(count)])
    return value


def shards(orbitals, potential):
    first = (apply_ham(orbitals, potential) - 5.5 * orbitals) / 4.5
    applied = apply_ham(first, potential)
    filtered = 2.0 * (applied - 5.5 * first) / 4.5 - orbitals
    count = filtered.shape[1] * filtered.shape[2] * filtered.shape[3]
    cells = count * lax.axis_size("gx") * lax.axis_size("gy")
    local_gram = (
        jnp.einsum(
            "kxyz,mxyz->km", filtered, filtered,
            precision=lax.Precision.HIGHEST, preferred_element_type=jnp.float32,
        )
        / cells
    )
    packed = local_gram.reshape(-1, 128)
    gram = butterfly_sum(butterfly_sum(packed, "gy"), "gx").reshape(local_gram.shape)
    factor, lower_inverse = factor_and_inverse(gram)
    basis = jnp.einsum(
        "mk,kxyz->mxyz", lower_inverse * jnp.sqrt(jnp.float32(cells)), filtered,
        precision=lax.Precision.HIGHEST, preferred_element_type=jnp.float32,
    )
    return (basis, factor)


def solution(mesh):
    return jax.shard_map(
        shards,
        mesh=mesh,
        in_specs=(P(None, "gx", "gy", None), P("gx", "gy", None)),
        out_specs=(P(None, "gx", "gy", None), P()),
        check_vma=False,
    )
```

```python
import jax
import jax.numpy as jnp
from jax import lax
from jax.experimental import pallas as pl
from jax.experimental.pallas import tpu as pltpu
from jax.sharding import PartitionSpec as P


def faces(cells, axis, dim, width):
    count = lax.axis_size(axis)
    size = cells.shape[dim]
    head = lax.slice_in_dim(cells, 0, width, axis=dim)
    tail = lax.slice_in_dim(cells, size - width, size, axis=dim)
    before = lax.ppermute(tail, axis, [(i, (i + 1) % count) for i in range(count)])
    after = lax.ppermute(head, axis, [((i + 1) % count, i) for i in range(count)])
    return jnp.concatenate([before, cells, after], axis=dim)


def apply_ham(core, pot):
    along_x = faces(core, "gx", 1, 2)
    along_y = faces(core, "gy", 2, 2)
    total = -7.5 * core
    total = total + 4.0 / 3.0 * (along_x[:, 3:-1] + along_x[:, 1:-3])
    total = total - 1.0 / 12.0 * (along_x[:, 4:] + along_x[:, :-4])
    total = total + 4.0 / 3.0 * (along_y[:, :, 3:-1] + along_y[:, :, 1:-3])
    total = total - 1.0 / 12.0 * (along_y[:, :, 4:] + along_y[:, :, :-4])
    size = core.shape[3]
    along_z = jnp.concatenate([core[..., size - 2:], core, core[..., :2]], axis=3)
    total = total + 4.0 / 3.0 * (along_z[..., 1:size + 1] + along_z[..., 3:size + 3])
    total = total - 1.0 / 12.0 * (along_z[..., :size] + along_z[..., 4:])
    return -0.5 * total + pot[None] * core


def factor_kernel(aug_ref, out_ref):
    order = aug_ref.shape[0]
    groups = order // 8
    blocks = [aug_ref[pl.ds(8 * i, 8), :] for i in range(groups)]
    sub = lax.broadcasted_iota(jnp.int32, blocks[0].shape, 0)
    lane = lax.broadcasted_iota(jnp.int32, blocks[0].shape, 1)
    for k in range(0, order, 2):
        home, place = divmod(k, 8)
        first_row = blocks[home][place:place + 1, :]
        first_inverse = 1.0 / first_row[:, k:k + 1]
        second_row = blocks[home][place + 1:place + 2, :]
        second_row = second_row - (second_row[:, k:k + 1] * first_inverse) * first_row
        second_inverse = 1.0 / second_row[:, k + 1:k + 2]
        coupling = first_row[:, k + 1:k + 2]
        for j in range(home, groups):
            block = blocks[j]
            first_column = block[:, k:k + 1] * first_inverse
            second_column = (block[:, k + 1:k + 2] - first_column * coupling) * second_inverse
            if j == home:
                first_column = jnp.where(sub[:, :1] > place, first_column, 0.0)
                second_column = jnp.where(sub[:, :1] > place + 1, second_column, 0.0)
            blocks[j] = block - first_column * first_row - second_column * second_row
    for i in range(groups):
        block = blocks[i]
        pivots = jnp.sum(jnp.where(lane == sub + 8 * i, block, 0.0), axis=1, keepdims=True)
        keep = (lane >= order) | (lane >= sub + 8 * i)
        out_ref[pl.ds(8 * i, 8), :] = jnp.where(keep, block / jnp.sqrt(pivots), 0.0)


def factor_and_inverse(gram):
    order = gram.shape[0]
    sym = 0.5 * (gram + gram.T)
    aug = jnp.concatenate([sym, jnp.eye(order, dtype=jnp.float32)], axis=1)
    out = pl.pallas_call(
        factor_kernel,
        out_shape=jax.ShapeDtypeStruct(aug.shape, jnp.float32),
        in_specs=[pl.BlockSpec(memory_space=pltpu.VMEM)],
        out_specs=pl.BlockSpec(memory_space=pltpu.VMEM),
    )(aug)
    return out[:, :order], out[:, order:]


def ring_rounds(stride):
    def flip(i):
        return i ^ stride

    def mirror(i):
        return i + (3 - 2 * ((i // stride) % 4)) * stride

    return [flip, mirror]


def butterfly_sum(value, axis):
    count = lax.axis_size(axis)
    if count & (count - 1):
        return lax.psum(value, axis)
    if count == 32:
        rounds = [lambda i: i ^ 1] + ring_rounds(2) + ring_rounds(8)
    else:
        rounds = [lambda i, mask=1 << b: i ^ mask for b in range(count.bit_length() - 1)]
    for partner in rounds:
        value = value + lax.ppermute(value, axis, [(i, partner(i)) for i in range(count)])
    return value


def shards(orbitals, potential):
    first = (apply_ham(orbitals, potential) - 5.5 * orbitals) / 4.5
    applied = apply_ham(first, potential)
    filtered = 2.0 * (applied - 5.5 * first) / 4.5 - orbitals
    count = filtered.shape[1] * filtered.shape[2] * filtered.shape[3]
    cells = count * lax.axis_size("gx") * lax.axis_size("gy")
    local_gram = (
        jnp.einsum(
            "kxyz,mxyz->km", filtered, filtered,
            precision=lax.Precision.HIGHEST, preferred_element_type=jnp.float32,
        )
        / cells
    )
    packed = local_gram.reshape(-1, 128)
    gram = butterfly_sum(butterfly_sum(packed, "gy"), "gx").reshape(local_gram.shape)
    factor, lower_inverse = factor_and_inverse(gram)
    basis = jnp.einsum(
        "mk,kxyz->mxyz", lower_inverse * jnp.sqrt(jnp.float32(cells)), filtered,
        precision=lax.Precision.HIGHEST, preferred_element_type=jnp.float32,
    )
    return (basis, factor)


def solution(mesh):
    return jax.shard_map(
        shards,
        mesh=mesh,
        in_specs=(P(None, "gx", "gy", None), P("gx", "gy", None)),
        out_specs=(P(None, "gx", "gy", None), P()),
        check_vma=False,
    )
```

```python
import jax
import jax.numpy as jnp
from jax import lax
from jax.experimental import pallas as pl
from jax.experimental.pallas import tpu as pltpu
from jax.sharding import PartitionSpec as P


def faces(cells, axis, dim, width):
    count = lax.axis_size(axis)
    size = cells.shape[dim]
    head = lax.slice_in_dim(cells, 0, width, axis=dim)
    tail = lax.slice_in_dim(cells, size - width, size, axis=dim)
    before = lax.ppermute(tail, axis, [(i, (i + 1) % count) for i in range(count)])
    after = lax.ppermute(head, axis, [((i + 1) % count, i) for i in range(count)])
    return jnp.concatenate([before, cells, after], axis=dim)


def apply_ham(core, pot, source=None):
    source = core if source is None else source
    along_x = faces(source, "gx", 1, 2)
    along_y = faces(source, "gy", 2, 2)
    if source is not core:
        along_x = jnp.concatenate([along_x[:, :2], core, along_x[:, -2:]], axis=1)
        along_y = jnp.concatenate([along_y[:, :, :2], core, along_y[:, :, -2:]], axis=2)
    total = -7.5 * core
    total = total + 4.0 / 3.0 * (along_x[:, 3:-1] + along_x[:, 1:-3])
    total = total - 1.0 / 12.0 * (along_x[:, 4:] + along_x[:, :-4])
    total = total + 4.0 / 3.0 * (along_y[:, :, 3:-1] + along_y[:, :, 1:-3])
    total = total - 1.0 / 12.0 * (along_y[:, :, 4:] + along_y[:, :, :-4])
    size = core.shape[3]
    along_z = jnp.concatenate([core[..., size - 2:], core, core[..., :2]], axis=3)
    total = total + 4.0 / 3.0 * (along_z[..., 1:size + 1] + along_z[..., 3:size + 3])
    total = total - 1.0 / 12.0 * (along_z[..., :size] + along_z[..., 4:])
    return -0.5 * total + pot[None] * core


def factor_kernel(aug_ref, out_ref):
    order = aug_ref.shape[0]
    groups = order // 8
    blocks = [aug_ref[pl.ds(8 * i, 8), :] for i in range(groups)]
    sub = lax.broadcasted_iota(jnp.int32, blocks[0].shape, 0)
    lane = lax.broadcasted_iota(jnp.int32, blocks[0].shape, 1)
    for k in range(order):
        home, place = divmod(k, 8)
        row = blocks[home][place:place + 1, :]
        inverse = 1.0 / row[:, k:k + 1]
        for j in range(home, groups):
            block = blocks[j]
            column = block[:, k:k + 1] * inverse
            if j == home:
                column = jnp.where(sub[:, :1] > place, column, 0.0)
            blocks[j] = block - column * row
    for i in range(groups):
        block = blocks[i]
        pivots = jnp.sum(jnp.where(lane == sub + 8 * i, block, 0.0), axis=1, keepdims=True)
        keep = (lane >= order) | (lane >= sub + 8 * i)
        out_ref[pl.ds(8 * i, 8), :] = jnp.where(keep, block / jnp.sqrt(pivots), 0.0)


def factor_and_inverse(gram):
    order = gram.shape[0]
    sym = 0.5 * (gram + gram.T)
    aug = jnp.concatenate([sym, jnp.eye(order, dtype=jnp.float32)], axis=1)
    out = pl.pallas_call(
        factor_kernel,
        out_shape=jax.ShapeDtypeStruct(aug.shape, jnp.float32),
        in_specs=[pl.BlockSpec(memory_space=pltpu.VMEM)],
        out_specs=pl.BlockSpec(memory_space=pltpu.VMEM),
    )(aug)
    return out[:, :order], out[:, order:]


def ring_rounds(stride):
    def flip(i):
        return i ^ stride

    def mirror(i):
        return i + (3 - 2 * ((i // stride) % 4)) * stride

    return [flip, mirror]


def butterfly_sum(value, axis):
    count = lax.axis_size(axis)
    if count & (count - 1):
        return lax.psum(value, axis)
    if count == 32:
        rounds = [lambda i: i ^ 1] + ring_rounds(2) + ring_rounds(8)
    else:
        rounds = [lambda i, mask=1 << b: i ^ mask for b in range(count.bit_length() - 1)]
    for partner in rounds:
        value = value + lax.ppermute(value, axis, [(i, partner(i)) for i in range(count)])
    return value


def shards(orbitals, potential):
    orbitals_here = lax.optimization_barrier(orbitals)
    first = (apply_ham(orbitals_here, potential, orbitals) - 5.5 * orbitals_here) / 4.5
    applied = apply_ham(first, potential)
    filtered = 2.0 * (applied - 5.5 * first) / 4.5 - orbitals_here
    count = filtered.shape[1] * filtered.shape[2] * filtered.shape[3]
    cells = count * lax.axis_size("gx") * lax.axis_size("gy")
    local_gram = (
        jnp.einsum(
            "kxyz,mxyz->km", filtered, filtered,
            precision=lax.Precision.HIGHEST, preferred_element_type=jnp.float32,
        )
        / cells
    )
    packed = local_gram.reshape(-1, 128)
    gram = butterfly_sum(butterfly_sum(packed, "gy"), "gx").reshape(local_gram.shape)
    factor, lower_inverse = factor_and_inverse(gram)
    basis = jnp.einsum(
        "mk,kxyz->mxyz", lower_inverse * jnp.sqrt(jnp.float32(cells)), filtered,
        precision=lax.Precision.HIGHEST, preferred_element_type=jnp.float32,
    )
    return (basis, factor)


def solution(mesh):
    return jax.shard_map(
        shards,
        mesh=mesh,
        in_specs=(P(None, "gx", "gy", None), P("gx", "gy", None)),
        out_specs=(P(None, "gx", "gy", None), P()),
        check_vma=False,
    )
```

```python
import jax
import jax.numpy as jnp
from jax import lax
from jax.experimental import pallas as pl
from jax.experimental.pallas import tpu as pltpu
from jax.sharding import PartitionSpec as P


def faces(cells, axis, dim, width):
    count = lax.axis_size(axis)
    size = cells.shape[dim]
    head = lax.slice_in_dim(cells, 0, width, axis=dim)
    tail = lax.slice_in_dim(cells, size - width, size, axis=dim)
    before = lax.ppermute(tail, axis, [(i, (i + 1) % count) for i in range(count)])
    after = lax.ppermute(head, axis, [((i + 1) % count, i) for i in range(count)])
    return jnp.concatenate([before, cells, after], axis=dim)


def apply_ham(core, pot, source=None):
    source = core if source is None else source
    along_x = faces(source, "gx", 1, 2)
    along_y = faces(source, "gy", 2, 2)
    if source is not core:
        along_x = jnp.concatenate([along_x[:, :2], core, along_x[:, -2:]], axis=1)
        along_y = jnp.concatenate([along_y[:, :, :2], core, along_y[:, :, -2:]], axis=2)
    total = -7.5 * core
    total = total + 4.0 / 3.0 * (along_x[:, 3:-1] + along_x[:, 1:-3])
    total = total - 1.0 / 12.0 * (along_x[:, 4:] + along_x[:, :-4])
    total = total + 4.0 / 3.0 * (along_y[:, :, 3:-1] + along_y[:, :, 1:-3])
    total = total - 1.0 / 12.0 * (along_y[:, :, 4:] + along_y[:, :, :-4])
    size = core.shape[3]
    along_z = jnp.concatenate([core[..., size - 2:], core, core[..., :2]], axis=3)
    total = total + 4.0 / 3.0 * (along_z[..., 1:size + 1] + along_z[..., 3:size + 3])
    total = total - 1.0 / 12.0 * (along_z[..., :size] + along_z[..., 4:])
    return -0.5 * total + pot[None] * core


def factor_kernel(aug_ref, out_ref):
    order = aug_ref.shape[0]
    groups = order // 8
    blocks = [aug_ref[pl.ds(8 * i, 8), :] for i in range(groups)]
    sub = lax.broadcasted_iota(jnp.int32, blocks[0].shape, 0)
    lane = lax.broadcasted_iota(jnp.int32, blocks[0].shape, 1)
    for k in range(order):
        home, place = divmod(k, 8)
        row = blocks[home][place:place + 1, :]
        inverse = 1.0 / row[:, k:k + 1]
        for j in range(home, groups):
            block = blocks[j]
            column = block[:, k:k + 1] * inverse
            if j == home:
                column = jnp.where(sub[:, :1] > place, column, 0.0)
            blocks[j] = block - column * row
    for i in range(groups):
        block = blocks[i]
        pivots = jnp.sum(jnp.where(lane == sub + 8 * i, block, 0.0), axis=1, keepdims=True)
        keep = (lane >= order) | (lane >= sub + 8 * i)
        out_ref[pl.ds(8 * i, 8), :] = jnp.where(keep, block / jnp.sqrt(pivots), 0.0)


def factor_and_inverse(gram):
    order = gram.shape[0]
    sym = 0.5 * (gram + gram.T)
    aug = jnp.concatenate([sym, jnp.eye(order, dtype=jnp.float32)], axis=1)
    out = pl.pallas_call(
        factor_kernel,
        out_shape=jax.ShapeDtypeStruct(aug.shape, jnp.float32),
        in_specs=[pl.BlockSpec(memory_space=pltpu.VMEM)],
        out_specs=pl.BlockSpec(memory_space=pltpu.VMEM),
    )(aug)
    return out[:, :order], out[:, order:]


def ring_rounds(stride):
    def flip(i):
        return i ^ stride

    def mirror(i):
        return i + (3 - 2 * ((i // stride) % 4)) * stride

    return [flip, mirror]


def butterfly_sum(value, axis):
    count = lax.axis_size(axis)
    if count & (count - 1):
        return lax.psum(value, axis)
    if count == 32:
        rounds = [lambda i: i ^ 1] + ring_rounds(2) + ring_rounds(8)
    elif count == 8:
        rounds = [lambda i: i ^ 1] + ring_rounds(2)
    else:
        rounds = [lambda i, mask=1 << b: i ^ mask for b in range(count.bit_length() - 1)]
    for partner in rounds:
        value = value + lax.ppermute(value, axis, [(i, partner(i)) for i in range(count)])
    return value


def shards(orbitals, potential):
    orbitals_here = lax.optimization_barrier(orbitals)
    first = (apply_ham(orbitals_here, potential, orbitals) - 5.5 * orbitals_here) / 4.5
    applied = apply_ham(first, potential)
    filtered = 2.0 * (applied - 5.5 * first) / 4.5 - orbitals_here
    count = filtered.shape[1] * filtered.shape[2] * filtered.shape[3]
    cells = count * lax.axis_size("gx") * lax.axis_size("gy")
    local_gram = (
        jnp.einsum(
            "kxyz,mxyz->km", filtered, filtered,
            precision=lax.Precision.HIGHEST, preferred_element_type=jnp.float32,
        )
        / cells
    )
    packed = local_gram.reshape(-1, 128)
    gram = butterfly_sum(butterfly_sum(packed, "gy"), "gx").reshape(local_gram.shape)
    factor, lower_inverse = factor_and_inverse(gram)
    basis = jnp.einsum(
        "mk,kxyz->mxyz", lower_inverse * jnp.sqrt(jnp.float32(cells)), filtered,
        precision=lax.Precision.HIGHEST, preferred_element_type=jnp.float32,
    )
    return (basis, factor)


def solution(mesh):
    return jax.shard_map(
        shards,
        mesh=mesh,
        in_specs=(P(None, "gx", "gy", None), P("gx", "gy", None)),
        out_specs=(P(None, "gx", "gy", None), P()),
        check_vma=False,
    )
```

```python
import jax
import jax.numpy as jnp
from jax import lax
from jax.experimental import pallas as pl
from jax.experimental.pallas import tpu as pltpu
from jax.sharding import PartitionSpec as P


def faces(cells, axis, dim, width):
    count = lax.axis_size(axis)
    size = cells.shape[dim]
    head = lax.slice_in_dim(cells, 0, width, axis=dim)
    tail = lax.slice_in_dim(cells, size - width, size, axis=dim)
    before = lax.ppermute(tail, axis, [(i, (i + 1) % count) for i in range(count)])
    after = lax.ppermute(head, axis, [((i + 1) % count, i) for i in range(count)])
    return jnp.concatenate([before, cells, after], axis=dim)


def apply_ham(core, pot, source=None):
    source = core if source is None else source
    along_x = faces(source, "gx", 1, 2)
    along_y = faces(source, "gy", 2, 2)
    if source is not core:
        along_x = jnp.concatenate([along_x[:, :2], core, along_x[:, -2:]], axis=1)
        along_y = jnp.concatenate([along_y[:, :, :2], core, along_y[:, :, -2:]], axis=2)
    size = core.shape[3]
    along_z = jnp.concatenate([core[..., size - 2:], core, core[..., :2]], axis=3)
    local = -7.5 * core
    local = local + 4.0 / 3.0 * (along_z[..., 1:size + 1] + along_z[..., 3:size + 3])
    local = local - 1.0 / 12.0 * (along_z[..., :size] + along_z[..., 4:])
    total = lax.optimization_barrier(local)
    total = total + 4.0 / 3.0 * (along_x[:, 3:-1] + along_x[:, 1:-3])
    total = total - 1.0 / 12.0 * (along_x[:, 4:] + along_x[:, :-4])
    total = total + 4.0 / 3.0 * (along_y[:, :, 3:-1] + along_y[:, :, 1:-3])
    total = total - 1.0 / 12.0 * (along_y[:, :, 4:] + along_y[:, :, :-4])
    return -0.5 * total + pot[None] * core


def factor_kernel(aug_ref, out_ref):
    order = aug_ref.shape[0]
    groups = order // 8
    blocks = [aug_ref[pl.ds(8 * i, 8), :] for i in range(groups)]
    sub = lax.broadcasted_iota(jnp.int32, blocks[0].shape, 0)
    lane = lax.broadcasted_iota(jnp.int32, blocks[0].shape, 1)
    for k in range(order):
        home, place = divmod(k, 8)
        row = blocks[home][place:place + 1, :]
        inverse = 1.0 / row[:, k:k + 1]
        for j in range(home, groups):
            block = blocks[j]
            column = block[:, k:k + 1] * inverse
            if j == home:
                column = jnp.where(sub[:, :1] > place, column, 0.0)
            blocks[j] = block - column * row
    for i in range(groups):
        block = blocks[i]
        pivots = jnp.sum(jnp.where(lane == sub + 8 * i, block, 0.0), axis=1, keepdims=True)
        keep = (lane >= order) | (lane >= sub + 8 * i)
        out_ref[pl.ds(8 * i, 8), :] = jnp.where(keep, block / jnp.sqrt(pivots), 0.0)


def factor_and_inverse(gram):
    order = gram.shape[0]
    sym = 0.5 * (gram + gram.T)
    aug = jnp.concatenate([sym, jnp.eye(order, dtype=jnp.float32)], axis=1)
    out = pl.pallas_call(
        factor_kernel,
        out_shape=jax.ShapeDtypeStruct(aug.shape, jnp.float32),
        in_specs=[pl.BlockSpec(memory_space=pltpu.VMEM)],
        out_specs=pl.BlockSpec(memory_space=pltpu.VMEM),
    )(aug)
    return out[:, :order], out[:, order:]


def ring_rounds(stride):
    def flip(i):
        return i ^ stride

    def mirror(i):
        return i + (3 - 2 * ((i // stride) % 4)) * stride

    return [flip, mirror]


def butterfly_sum(value, axis):
    count = lax.axis_size(axis)
    if count & (count - 1):
        return lax.psum(value, axis)
    if count == 32:
        rounds = [lambda i: i ^ 1] + ring_rounds(2) + ring_rounds(8)
    elif count == 8:
        rounds = [lambda i: i ^ 1] + ring_rounds(2)
    else:
        rounds = [lambda i, mask=1 << b: i ^ mask for b in range(count.bit_length() - 1)]
    for partner in rounds:
        value = value + lax.ppermute(value, axis, [(i, partner(i)) for i in range(count)])
    return value


def shards(orbitals, potential):
    orbitals_here = lax.optimization_barrier(orbitals)
    first = (apply_ham(orbitals_here, potential, orbitals) - 5.5 * orbitals_here) / 4.5
    applied = apply_ham(first, potential)
    filtered = 2.0 * (applied - 5.5 * first) / 4.5 - orbitals_here
    count = filtered.shape[1] * filtered.shape[2] * filtered.shape[3]
    cells = count * lax.axis_size("gx") * lax.axis_size("gy")
    local_gram = (
        jnp.einsum(
            "kxyz,mxyz->km", filtered, filtered,
            precision=lax.Precision.HIGHEST, preferred_element_type=jnp.float32,
        )
        / cells
    )
    packed = local_gram.reshape(-1, 128)
    gram = butterfly_sum(butterfly_sum(packed, "gy"), "gx").reshape(local_gram.shape)
    factor, lower_inverse = factor_and_inverse(gram)
    basis = jnp.einsum(
        "mk,kxyz->mxyz", lower_inverse * jnp.sqrt(jnp.float32(cells)), filtered,
        precision=lax.Precision.HIGHEST, preferred_element_type=jnp.float32,
    )
    return (basis, factor)


def solution(mesh):
    return jax.shard_map(
        shards,
        mesh=mesh,
        in_specs=(P(None, "gx", "gy", None), P("gx", "gy", None)),
        out_specs=(P(None, "gx", "gy", None), P()),
        check_vma=False,
    )
```

```python
import jax
import jax.numpy as jnp
from jax import lax
from jax.experimental import pallas as pl
from jax.experimental.pallas import tpu as pltpu
from jax.sharding import PartitionSpec as P


def faces(cells, axis, dim, width):
    count = lax.axis_size(axis)
    size = cells.shape[dim]
    head = lax.slice_in_dim(cells, 0, width, axis=dim)
    tail = lax.slice_in_dim(cells, size - width, size, axis=dim)
    before = lax.ppermute(tail, axis, [(i, (i + 1) % count) for i in range(count)])
    after = lax.ppermute(head, axis, [((i + 1) % count, i) for i in range(count)])
    return jnp.concatenate([before, cells, after], axis=dim)


def apply_ham(core, pot, source=None):
    source = core if source is None else source
    along_x = faces(source, "gx", 1, 2)
    along_y = faces(source, "gy", 2, 2)
    if source is not core:
        along_x = jnp.concatenate([along_x[:, :2], core, along_x[:, -2:]], axis=1)
        along_y = jnp.concatenate([along_y[:, :, :2], core, along_y[:, :, -2:]], axis=2)
    size = core.shape[3]
    along_z = jnp.concatenate([core[..., size - 2:], core, core[..., :2]], axis=3)
    local = -7.5 * core
    local = local + 4.0 / 3.0 * (along_z[..., 1:size + 1] + along_z[..., 3:size + 3])
    local = local - 1.0 / 12.0 * (along_z[..., :size] + along_z[..., 4:])
    total = lax.optimization_barrier(local)
    total = total + 4.0 / 3.0 * (along_x[:, 3:-1] + along_x[:, 1:-3])
    total = total - 1.0 / 12.0 * (along_x[:, 4:] + along_x[:, :-4])
    total = total + 4.0 / 3.0 * (along_y[:, :, 3:-1] + along_y[:, :, 1:-3])
    total = total - 1.0 / 12.0 * (along_y[:, :, 4:] + along_y[:, :, :-4])
    return -0.5 * total + pot[None] * core


def factor_kernel(aug_ref, out_ref):
    order = aug_ref.shape[0]
    groups = order // 8
    blocks = [aug_ref[pl.ds(8 * i, 8), :] for i in range(groups)]
    sub = lax.broadcasted_iota(jnp.int32, blocks[0].shape, 0)
    lane = lax.broadcasted_iota(jnp.int32, blocks[0].shape, 1)
    for k in range(order):
        home, place = divmod(k, 8)
        row = blocks[home][place:place + 1, :]
        inverse = 1.0 / row[:, k:k + 1]
        for j in range(home, groups):
            block = blocks[j]
            column = block[:, k:k + 1] * inverse
            if j == home:
                column = jnp.where(sub[:, :1] > place, column, 0.0)
            blocks[j] = block - column * row
    for i in range(groups):
        block = blocks[i]
        pivots = jnp.sum(jnp.where(lane == sub + 8 * i, block, 0.0), axis=1, keepdims=True)
        keep = (lane >= order) | (lane >= sub + 8 * i)
        out_ref[pl.ds(8 * i, 8), :] = jnp.where(keep, block / jnp.sqrt(pivots), 0.0)


def factor_and_inverse(gram):
    order = gram.shape[0]
    sym = 0.5 * (gram + gram.T)
    aug = jnp.concatenate([sym, jnp.eye(order, dtype=jnp.float32)], axis=1)
    out = pl.pallas_call(
        factor_kernel,
        out_shape=jax.ShapeDtypeStruct(aug.shape, jnp.float32),
        in_specs=[pl.BlockSpec(memory_space=pltpu.VMEM)],
        out_specs=pl.BlockSpec(memory_space=pltpu.VMEM),
    )(aug)
    return out[:, :order], out[:, order:]


def ring_rounds(stride):
    def flip(i):
        return i ^ stride

    def mirror(i):
        return i + (3 - 2 * ((i // stride) % 4)) * stride

    return [flip, mirror]


def butterfly_sum(value, axis):
    count = lax.axis_size(axis)
    if count & (count - 1):
        return lax.psum(value, axis)
    if count == 32:
        rounds = [lambda i: i ^ 1] + ring_rounds(2) + ring_rounds(8)
    elif count == 8:
        rounds = [lambda i: i ^ 1] + ring_rounds(2)
    else:
        rounds = [lambda i, mask=1 << b: i ^ mask for b in range(count.bit_length() - 1)]
    for partner in rounds:
        value = value + lax.ppermute(value, axis, [(i, partner(i)) for i in range(count)])
    return value


def shards(orbitals, potential):
    orbitals_here = lax.optimization_barrier(orbitals)
    first = (apply_ham(orbitals_here, potential, orbitals) - 5.5 * orbitals_here) / 4.5
    applied = apply_ham(first, potential)
    filtered = 2.0 * (applied - 5.5 * first) / 4.5 - orbitals_here
    count = filtered.shape[1] * filtered.shape[2] * filtered.shape[3]
    cells = count * lax.axis_size("gx") * lax.axis_size("gy")
    local_gram = (
        jnp.einsum(
            "kxyz,mxyz->km", filtered, filtered,
            precision=lax.Precision.HIGHEST, preferred_element_type=jnp.float32,
        )
        / cells
    )
    packed = local_gram.reshape(-1, 128)
    gram = butterfly_sum(butterfly_sum(packed, "gx"), "gy").reshape(local_gram.shape)
    factor, lower_inverse = factor_and_inverse(gram)
    basis = jnp.einsum(
        "mk,kxyz->mxyz", lower_inverse * jnp.sqrt(jnp.float32(cells)), filtered,
        precision=lax.Precision.HIGHEST, preferred_element_type=jnp.float32,
    )
    return (basis, factor)


def solution(mesh):
    return jax.shard_map(
        shards,
        mesh=mesh,
        in_specs=(P(None, "gx", "gy", None), P("gx", "gy", None)),
        out_specs=(P(None, "gx", "gy", None), P()),
        check_vma=False,
    )
```

```python
import jax
import jax.numpy as jnp
from jax import lax
from jax.experimental import pallas as pl
from jax.experimental.pallas import tpu as pltpu
from jax.sharding import PartitionSpec as P


def faces(cells, axis, dim, width):
    count = lax.axis_size(axis)
    size = cells.shape[dim]
    head = lax.slice_in_dim(cells, 0, width, axis=dim)
    tail = lax.slice_in_dim(cells, size - width, size, axis=dim)
    before = lax.ppermute(tail, axis, [(i, (i + 1) % count) for i in range(count)])
    after = lax.ppermute(head, axis, [((i + 1) % count, i) for i in range(count)])
    return jnp.concatenate([before, cells, after], axis=dim)


def apply_ham(core, pot, source=None):
    source = core if source is None else source
    along_x = faces(source, "gx", 1, 2)
    along_y = faces(source, "gy", 2, 2)
    if source is not core:
        along_x = jnp.concatenate([along_x[:, :2], core, along_x[:, -2:]], axis=1)
        along_y = jnp.concatenate([along_y[:, :, :2], core, along_y[:, :, -2:]], axis=2)
    size = core.shape[3]
    along_z = jnp.concatenate([core[..., size - 2:], core, core[..., :2]], axis=3)
    local = -7.5 * core
    local = local + 4.0 / 3.0 * (along_z[..., 1:size + 1] + along_z[..., 3:size + 3])
    local = local - 1.0 / 12.0 * (along_z[..., :size] + along_z[..., 4:])
    total = lax.optimization_barrier(local)
    total = total + 4.0 / 3.0 * (along_x[:, 3:-1] + along_x[:, 1:-3])
    total = total - 1.0 / 12.0 * (along_x[:, 4:] + along_x[:, :-4])
    total = total + 4.0 / 3.0 * (along_y[:, :, 3:-1] + along_y[:, :, 1:-3])
    total = total - 1.0 / 12.0 * (along_y[:, :, 4:] + along_y[:, :, :-4])
    return -0.5 * total + pot[None] * core


def factor_kernel(gram_ref, flipped_ref, factor_ref, inverse_ref):
    order = gram_ref.shape[0]
    groups = order // 8
    sub = lax.broadcasted_iota(jnp.int32, (8, order), 0)
    lane = lax.broadcasted_iota(jnp.int32, (8, order), 1)
    left = [
        0.5 * (gram_ref[pl.ds(8 * i, 8), :] + flipped_ref[pl.ds(8 * i, 8), :])
        for i in range(groups)
    ]
    right = [jnp.where(lane == sub + 8 * i, 1.0, 0.0) for i in range(groups)]
    for k in range(order):
        home, place = divmod(k, 8)
        row = left[home][place:place + 1, :]
        row_right = right[home][place:place + 1, :]
        inverse = 1.0 / row[:, k:k + 1]
        for j in range(home, groups):
            column = left[j][:, k:k + 1] * inverse
            if j == home:
                column = jnp.where(sub[:, :1] > place, column, 0.0)
            left[j] = left[j] - column * row
            right[j] = right[j] - column * row_right
    for i in range(groups):
        pivots = jnp.sum(jnp.where(lane == sub + 8 * i, left[i], 0.0), axis=1, keepdims=True)
        scale = 1.0 / jnp.sqrt(pivots)
        factor_ref[pl.ds(8 * i, 8), :] = jnp.where(lane >= sub + 8 * i, left[i] * scale, 0.0)
        inverse_ref[pl.ds(8 * i, 8), :] = right[i] * scale


def factor_and_inverse(gram):
    shape = jax.ShapeDtypeStruct(gram.shape, jnp.float32)
    return pl.pallas_call(
        factor_kernel,
        out_shape=(shape, shape),
        in_specs=[pl.BlockSpec(memory_space=pltpu.VMEM)] * 2,
        out_specs=(pl.BlockSpec(memory_space=pltpu.VMEM),) * 2,
    )(gram, gram.T)


def ring_rounds(stride):
    def flip(i):
        return i ^ stride

    def mirror(i):
        return i + (3 - 2 * ((i // stride) % 4)) * stride

    return [flip, mirror]


def butterfly_sum(value, axis):
    count = lax.axis_size(axis)
    if count & (count - 1):
        return lax.psum(value, axis)
    if count == 32:
        rounds = [lambda i: i ^ 1] + ring_rounds(2) + ring_rounds(8)
    elif count == 8:
        rounds = [lambda i: i ^ 1] + ring_rounds(2)
    else:
        rounds = [lambda i, mask=1 << b: i ^ mask for b in range(count.bit_length() - 1)]
    for partner in rounds:
        value = value + lax.ppermute(value, axis, [(i, partner(i)) for i in range(count)])
    return value


def shards(orbitals, potential):
    orbitals_here = lax.optimization_barrier(orbitals)
    first = (apply_ham(orbitals_here, potential, orbitals) - 5.5 * orbitals_here) / 4.5
    applied = apply_ham(first, potential)
    filtered = 2.0 * (applied - 5.5 * first) / 4.5 - orbitals_here
    count = filtered.shape[1] * filtered.shape[2] * filtered.shape[3]
    cells = count * lax.axis_size("gx") * lax.axis_size("gy")
    local_gram = (
        jnp.einsum(
            "kxyz,mxyz->km", filtered, filtered,
            precision=lax.Precision.HIGHEST, preferred_element_type=jnp.float32,
        )
        / cells
    )
    packed = local_gram.reshape(-1, 128)
    gram = butterfly_sum(butterfly_sum(packed, "gy"), "gx").reshape(local_gram.shape)
    factor, lower_inverse = factor_and_inverse(gram)
    basis = jnp.einsum(
        "mk,kxyz->mxyz", lower_inverse * jnp.sqrt(jnp.float32(cells)), filtered,
        precision=lax.Precision.HIGHEST, preferred_element_type=jnp.float32,
    )
    return (basis, factor)


def solution(mesh):
    return jax.shard_map(
        shards,
        mesh=mesh,
        in_specs=(P(None, "gx", "gy", None), P("gx", "gy", None)),
        out_specs=(P(None, "gx", "gy", None), P()),
        check_vma=False,
    )
```

```python
import jax
import jax.numpy as jnp
from jax import lax
from jax.experimental import pallas as pl
from jax.experimental.pallas import tpu as pltpu
from jax.sharding import PartitionSpec as P


def faces(cells, axis, dim, width):
    count = lax.axis_size(axis)
    size = cells.shape[dim]
    head = lax.slice_in_dim(cells, 0, width, axis=dim)
    tail = lax.slice_in_dim(cells, size - width, size, axis=dim)
    before = lax.ppermute(tail, axis, [(i, (i + 1) % count) for i in range(count)])
    after = lax.ppermute(head, axis, [((i + 1) % count, i) for i in range(count)])
    return jnp.concatenate([before, cells, after], axis=dim)


def apply_ham(core, pot, source=None):
    source = core if source is None else source
    along_x = faces(source, "gx", 1, 2)
    along_y = faces(source, "gy", 2, 2)
    if source is not core:
        along_x = jnp.concatenate([along_x[:, :2], core, along_x[:, -2:]], axis=1)
        along_y = jnp.concatenate([along_y[:, :, :2], core, along_y[:, :, -2:]], axis=2)
    size = core.shape[3]
    along_z = jnp.concatenate([core[..., size - 2:], core, core[..., :2]], axis=3)
    local = -7.5 * core
    local = local + 4.0 / 3.0 * (along_z[..., 1:size + 1] + along_z[..., 3:size + 3])
    local = local - 1.0 / 12.0 * (along_z[..., :size] + along_z[..., 4:])
    total = lax.optimization_barrier(local)
    total = total + 4.0 / 3.0 * (along_x[:, 3:-1] + along_x[:, 1:-3])
    total = total - 1.0 / 12.0 * (along_x[:, 4:] + along_x[:, :-4])
    total = total + 4.0 / 3.0 * (along_y[:, :, 3:-1] + along_y[:, :, 1:-3])
    total = total - 1.0 / 12.0 * (along_y[:, :, 4:] + along_y[:, :, :-4])
    return -0.5 * total + pot[None] * core


def factor_kernel(gram_ref, factor_ref, inverse_ref):
    order = gram_ref.shape[0]
    groups = order // 8
    sub = lax.broadcasted_iota(jnp.int32, (8, order), 0)
    lane = lax.broadcasted_iota(jnp.int32, (8, order), 1)
    gram = gram_ref[...]
    sym = 0.5 * (gram + gram.T)
    left = [sym[8 * i:8 * i + 8, :] for i in range(groups)]
    right = [jnp.where(lane == sub + 8 * i, 1.0, 0.0) for i in range(groups)]
    for k in range(order):
        home, place = divmod(k, 8)
        row = left[home][place:place + 1, :]
        row_right = right[home][place:place + 1, :]
        inverse = 1.0 / row[:, k:k + 1]
        for j in range(home, groups):
            column = left[j][:, k:k + 1] * inverse
            if j == home:
                column = jnp.where(sub[:, :1] > place, column, 0.0)
            left[j] = left[j] - column * row
            right[j] = right[j] - column * row_right
    for i in range(groups):
        pivots = jnp.sum(jnp.where(lane == sub + 8 * i, left[i], 0.0), axis=1, keepdims=True)
        scale = 1.0 / jnp.sqrt(pivots)
        factor_ref[pl.ds(8 * i, 8), :] = jnp.where(lane >= sub + 8 * i, left[i] * scale, 0.0)
        inverse_ref[pl.ds(8 * i, 8), :] = right[i] * scale


def factor_and_inverse(gram):
    shape = jax.ShapeDtypeStruct(gram.shape, jnp.float32)
    return pl.pallas_call(
        factor_kernel,
        out_shape=(shape, shape),
        in_specs=[pl.BlockSpec(memory_space=pltpu.VMEM)],
        out_specs=(pl.BlockSpec(memory_space=pltpu.VMEM),) * 2,
    )(gram)


def ring_rounds(stride):
    def flip(i):
        return i ^ stride

    def mirror(i):
        return i + (3 - 2 * ((i // stride) % 4)) * stride

    return [flip, mirror]


def butterfly_sum(value, axis):
    count = lax.axis_size(axis)
    if count & (count - 1):
        return lax.psum(value, axis)
    if count == 32:
        rounds = [lambda i: i ^ 1] + ring_rounds(2) + ring_rounds(8)
    elif count == 8:
        rounds = [lambda i: i ^ 1] + ring_rounds(2)
    else:
        rounds = [lambda i, mask=1 << b: i ^ mask for b in range(count.bit_length() - 1)]
    for partner in rounds:
        value = value + lax.ppermute(value, axis, [(i, partner(i)) for i in range(count)])
    return value


def shards(orbitals, potential):
    orbitals_here = lax.optimization_barrier(orbitals)
    first = (apply_ham(orbitals_here, potential, orbitals) - 5.5 * orbitals_here) / 4.5
    applied = apply_ham(first, potential)
    filtered = 2.0 * (applied - 5.5 * first) / 4.5 - orbitals_here
    count = filtered.shape[1] * filtered.shape[2] * filtered.shape[3]
    cells = count * lax.axis_size("gx") * lax.axis_size("gy")
    local_gram = (
        jnp.einsum(
            "kxyz,mxyz->km", filtered, filtered,
            precision=lax.Precision.HIGHEST, preferred_element_type=jnp.float32,
        )
        / cells
    )
    packed = local_gram.reshape(-1, 128)
    gram = butterfly_sum(butterfly_sum(packed, "gy"), "gx").reshape(local_gram.shape)
    factor, lower_inverse = factor_and_inverse(gram)
    basis = jnp.einsum(
        "mk,kxyz->mxyz", lower_inverse * jnp.sqrt(jnp.float32(cells)), filtered,
        precision=lax.Precision.HIGHEST, preferred_element_type=jnp.float32,
    )
    return (basis, factor)


def solution(mesh):
    return jax.shard_map(
        shards,
        mesh=mesh,
        in_specs=(P(None, "gx", "gy", None), P("gx", "gy", None)),
        out_specs=(P(None, "gx", "gy", None), P()),
        check_vma=False,
    )
```

```python
import jax
import jax.numpy as jnp
from jax import lax
from jax.experimental import pallas as pl
from jax.experimental.pallas import tpu as pltpu
from jax.sharding import PartitionSpec as P


def faces(cells, axis, dim, width):
    count = lax.axis_size(axis)
    size = cells.shape[dim]
    head = lax.slice_in_dim(cells, 0, width, axis=dim)
    tail = lax.slice_in_dim(cells, size - width, size, axis=dim)
    before = lax.ppermute(tail, axis, [(i, (i + 1) % count) for i in range(count)])
    after = lax.ppermute(head, axis, [((i + 1) % count, i) for i in range(count)])
    return jnp.concatenate([before, cells, after], axis=dim)


def apply_ham(core, pot, source=None):
    source = core if source is None else source
    along_x = faces(source, "gx", 1, 2)
    along_y = faces(source, "gy", 2, 2)
    if source is not core:
        along_x = jnp.concatenate([along_x[:, :2], core, along_x[:, -2:]], axis=1)
        along_y = jnp.concatenate([along_y[:, :, :2], core, along_y[:, :, -2:]], axis=2)
    size = core.shape[3]
    along_z = jnp.concatenate([core[..., size - 2:], core, core[..., :2]], axis=3)
    local = -7.5 * core
    local = local + 4.0 / 3.0 * (along_z[..., 1:size + 1] + along_z[..., 3:size + 3])
    local = local - 1.0 / 12.0 * (along_z[..., :size] + along_z[..., 4:])
    total = lax.optimization_barrier(local)
    total = total + 4.0 / 3.0 * (along_x[:, 3:-1] + along_x[:, 1:-3])
    total = total - 1.0 / 12.0 * (along_x[:, 4:] + along_x[:, :-4])
    total = total + 4.0 / 3.0 * (along_y[:, :, 3:-1] + along_y[:, :, 1:-3])
    total = total - 1.0 / 12.0 * (along_y[:, :, 4:] + along_y[:, :, :-4])
    return -0.5 * total + pot[None] * core


def factor_kernel(gram_ref, factor_ref, inverse_ref):
    half = gram_ref.shape[1] // 2
    order = gram_ref.shape[0] * gram_ref.shape[1] // half
    groups = order // 8
    sub = lax.broadcasted_iota(jnp.int32, (8, order), 0)
    lane = lax.broadcasted_iota(jnp.int32, (8, order), 1)
    packed = gram_ref[...]
    gram = jnp.concatenate(
        [piece for r in range(packed.shape[0]) for piece in (packed[r:r + 1, :half], packed[r:r + 1, half:])],
        axis=0,
    )
    sym = 0.5 * (gram + gram.T)
    left = [sym[8 * i:8 * i + 8, :] for i in range(groups)]
    right = [jnp.where(lane == sub + 8 * i, 1.0, 0.0) for i in range(groups)]
    for k in range(order):
        home, place = divmod(k, 8)
        row = left[home][place:place + 1, :]
        row_right = right[home][place:place + 1, :]
        inverse = 1.0 / row[:, k:k + 1]
        for j in range(home, groups):
            column = left[j][:, k:k + 1] * inverse
            if j == home:
                column = jnp.where(sub[:, :1] > place, column, 0.0)
            left[j] = left[j] - column * row
            right[j] = right[j] - column * row_right
    for i in range(groups):
        pivots = jnp.sum(jnp.where(lane == sub + 8 * i, left[i], 0.0), axis=1, keepdims=True)
        scale = 1.0 / jnp.sqrt(pivots)
        factor_ref[pl.ds(8 * i, 8), :] = jnp.where(lane >= sub + 8 * i, left[i] * scale, 0.0)
        inverse_ref[pl.ds(8 * i, 8), :] = right[i] * scale


def factor_and_inverse(packed, order):
    shape = jax.ShapeDtypeStruct((order, order), jnp.float32)
    return pl.pallas_call(
        factor_kernel,
        out_shape=(shape, shape),
        in_specs=[pl.BlockSpec(memory_space=pltpu.VMEM)],
        out_specs=(pl.BlockSpec(memory_space=pltpu.VMEM),) * 2,
    )(packed)


def ring_rounds(stride):
    def flip(i):
        return i ^ stride

    def mirror(i):
        return i + (3 - 2 * ((i // stride) % 4)) * stride

    return [flip, mirror]


def butterfly_sum(value, axis):
    count = lax.axis_size(axis)
    if count & (count - 1):
        return lax.psum(value, axis)
    if count == 32:
        rounds = [lambda i: i ^ 1] + ring_rounds(2) + ring_rounds(8)
    elif count == 8:
        rounds = [lambda i: i ^ 1] + ring_rounds(2)
    else:
        rounds = [lambda i, mask=1 << b: i ^ mask for b in range(count.bit_length() - 1)]
    for partner in rounds:
        value = value + lax.ppermute(value, axis, [(i, partner(i)) for i in range(count)])
    return value


def shards(orbitals, potential):
    orbitals_here = lax.optimization_barrier(orbitals)
    first = (apply_ham(orbitals_here, potential, orbitals) - 5.5 * orbitals_here) / 4.5
    applied = apply_ham(first, potential)
    filtered = 2.0 * (applied - 5.5 * first) / 4.5 - orbitals_here
    count = filtered.shape[1] * filtered.shape[2] * filtered.shape[3]
    cells = count * lax.axis_size("gx") * lax.axis_size("gy")
    local_gram = (
        jnp.einsum(
            "kxyz,mxyz->km", filtered, filtered,
            precision=lax.Precision.HIGHEST, preferred_element_type=jnp.float32,
        )
        / cells
    )
    packed = local_gram.reshape(-1, 128)
    gram = butterfly_sum(butterfly_sum(packed, "gy"), "gx")
    factor, lower_inverse = factor_and_inverse(gram, local_gram.shape[0])
    basis = jnp.einsum(
        "mk,kxyz->mxyz", lower_inverse * jnp.sqrt(jnp.float32(cells)), filtered,
        precision=lax.Precision.HIGHEST, preferred_element_type=jnp.float32,
    )
    return (basis, factor)


def solution(mesh):
    return jax.shard_map(
        shards,
        mesh=mesh,
        in_specs=(P(None, "gx", "gy", None), P("gx", "gy", None)),
        out_specs=(P(None, "gx", "gy", None), P()),
        check_vma=False,
    )
```

```python
import jax
import jax.numpy as jnp
from jax import lax
from jax.experimental import pallas as pl
from jax.experimental.pallas import tpu as pltpu
from jax.sharding import PartitionSpec as P


def faces(cells, axis, dim, width):
    count = lax.axis_size(axis)
    size = cells.shape[dim]
    head = lax.slice_in_dim(cells, 0, width, axis=dim)
    tail = lax.slice_in_dim(cells, size - width, size, axis=dim)
    before = lax.ppermute(tail, axis, [(i, (i + 1) % count) for i in range(count)])
    after = lax.ppermute(head, axis, [((i + 1) % count, i) for i in range(count)])
    return jnp.concatenate([before, cells, after], axis=dim)


def apply_ham(core, pot, source=None):
    source = core if source is None else source
    along_x = faces(source, "gx", 1, 2)
    along_y = faces(source, "gy", 2, 2)
    if source is not core:
        along_x = jnp.concatenate([along_x[:, :2], core, along_x[:, -2:]], axis=1)
        along_y = jnp.concatenate([along_y[:, :, :2], core, along_y[:, :, -2:]], axis=2)
    size = core.shape[3]
    along_z = jnp.concatenate([core[..., size - 2:], core, core[..., :2]], axis=3)
    local = -7.5 * core
    local = local + 4.0 / 3.0 * (along_z[..., 1:size + 1] + along_z[..., 3:size + 3])
    local = local - 1.0 / 12.0 * (along_z[..., :size] + along_z[..., 4:])
    total = lax.optimization_barrier(local)
    total = total + 4.0 / 3.0 * (along_x[:, 3:-1] + along_x[:, 1:-3])
    total = total - 1.0 / 12.0 * (along_x[:, 4:] + along_x[:, :-4])
    total = total + 4.0 / 3.0 * (along_y[:, :, 3:-1] + along_y[:, :, 1:-3])
    total = total - 1.0 / 12.0 * (along_y[:, :, 4:] + along_y[:, :, :-4])
    return -0.5 * total + pot[None] * core


def factor_kernel(gram_ref, received_ref, factor_ref, inverse_ref):
    half = gram_ref.shape[1] // 2
    order = gram_ref.shape[0] * gram_ref.shape[1] // half
    groups = order // 8
    sub = lax.broadcasted_iota(jnp.int32, (8, order), 0)
    lane = lax.broadcasted_iota(jnp.int32, (8, order), 1)
    packed = gram_ref[...] + received_ref[...]
    gram = jnp.concatenate(
        [piece for r in range(packed.shape[0]) for piece in (packed[r:r + 1, :half], packed[r:r + 1, half:])],
        axis=0,
    )
    sym = 0.5 * (gram + gram.T)
    left = [sym[8 * i:8 * i + 8, :] for i in range(groups)]
    right = [jnp.where(lane == sub + 8 * i, 1.0, 0.0) for i in range(groups)]
    for k in range(order):
        home, place = divmod(k, 8)
        row = left[home][place:place + 1, :]
        row_right = right[home][place:place + 1, :]
        inverse = 1.0 / row[:, k:k + 1]
        for j in range(home, groups):
            column = left[j][:, k:k + 1] * inverse
            if j == home:
                column = jnp.where(sub[:, :1] > place, column, 0.0)
            left[j] = left[j] - column * row
            right[j] = right[j] - column * row_right
    for i in range(groups):
        pivots = jnp.sum(jnp.where(lane == sub + 8 * i, left[i], 0.0), axis=1, keepdims=True)
        scale = 1.0 / jnp.sqrt(pivots)
        factor_ref[pl.ds(8 * i, 8), :] = jnp.where(lane >= sub + 8 * i, left[i] * scale, 0.0)
        inverse_ref[pl.ds(8 * i, 8), :] = right[i] * scale


def factor_and_inverse(packed, received, order):
    shape = jax.ShapeDtypeStruct((order, order), jnp.float32)
    return pl.pallas_call(
        factor_kernel,
        out_shape=(shape, shape),
        in_specs=[pl.BlockSpec(memory_space=pltpu.VMEM)] * 2,
        out_specs=(pl.BlockSpec(memory_space=pltpu.VMEM),) * 2,
    )(packed, received)


def ring_rounds(stride):
    def flip(i):
        return i ^ stride

    def mirror(i):
        return i + (3 - 2 * ((i // stride) % 4)) * stride

    return [flip, mirror]


def butterfly_sum(value, axis, open_last=False):
    count = lax.axis_size(axis)
    if count & (count - 1):
        total = lax.psum(value, axis)
        return (total, jnp.zeros_like(total)) if open_last else total
    if count == 32:
        rounds = [lambda i: i ^ 1] + ring_rounds(2) + ring_rounds(8)
    elif count == 8:
        rounds = [lambda i: i ^ 1] + ring_rounds(2)
    else:
        rounds = [lambda i, mask=1 << b: i ^ mask for b in range(count.bit_length() - 1)]
    for step, partner in enumerate(rounds):
        received = lax.ppermute(value, axis, [(i, partner(i)) for i in range(count)])
        if open_last and step == len(rounds) - 1:
            return value, received
        value = value + received
    return value


def shards(orbitals, potential):
    orbitals_here = lax.optimization_barrier(orbitals)
    first = (apply_ham(orbitals_here, potential, orbitals) - 5.5 * orbitals_here) / 4.5
    applied = apply_ham(first, potential)
    filtered = 2.0 * (applied - 5.5 * first) / 4.5 - orbitals_here
    count = filtered.shape[1] * filtered.shape[2] * filtered.shape[3]
    cells = count * lax.axis_size("gx") * lax.axis_size("gy")
    local_gram = (
        jnp.einsum(
            "kxyz,mxyz->km", filtered, filtered,
            precision=lax.Precision.HIGHEST, preferred_element_type=jnp.float32,
        )
        / cells
    )
    packed = local_gram.reshape(-1, 128)
    gram, received = butterfly_sum(butterfly_sum(packed, "gy"), "gx", open_last=True)
    factor, lower_inverse = factor_and_inverse(gram, received, local_gram.shape[0])
    basis = jnp.einsum(
        "mk,kxyz->mxyz", lower_inverse * jnp.sqrt(jnp.float32(cells)), filtered,
        precision=lax.Precision.HIGHEST, preferred_element_type=jnp.float32,
    )
    return (basis, factor)


def solution(mesh):
    return jax.shard_map(
        shards,
        mesh=mesh,
        in_specs=(P(None, "gx", "gy", None), P("gx", "gy", None)),
        out_specs=(P(None, "gx", "gy", None), P()),
        check_vma=False,
    )
```

```python
import jax
import jax.numpy as jnp
from jax import lax
from jax.experimental import pallas as pl
from jax.experimental.pallas import tpu as pltpu
from jax.sharding import PartitionSpec as P


def faces(cells, axis, dim, width):
    count = lax.axis_size(axis)
    size = cells.shape[dim]
    head = lax.slice_in_dim(cells, 0, width, axis=dim)
    tail = lax.slice_in_dim(cells, size - width, size, axis=dim)
    before = lax.ppermute(tail, axis, [(i, (i + 1) % count) for i in range(count)])
    after = lax.ppermute(head, axis, [((i + 1) % count, i) for i in range(count)])
    return jnp.concatenate([before, cells, after], axis=dim)


def apply_ham(core, pot, source=None):
    source = core if source is None else source
    along_x = faces(source, "gx", 1, 2)
    along_y = faces(source, "gy", 2, 2)
    if source is not core:
        along_x = jnp.concatenate([along_x[:, :2], core, along_x[:, -2:]], axis=1)
        along_y = jnp.concatenate([along_y[:, :, :2], core, along_y[:, :, -2:]], axis=2)
    size = core.shape[3]
    along_z = jnp.concatenate([core[..., size - 2:], core, core[..., :2]], axis=3)
    local = -7.5 * core
    local = local + 4.0 / 3.0 * (along_z[..., 1:size + 1] + along_z[..., 3:size + 3])
    local = local - 1.0 / 12.0 * (along_z[..., :size] + along_z[..., 4:])
    shifted = lax.optimization_barrier(-0.5 * local + pot[None] * core - 5.5 * core)
    total = 4.0 / 3.0 * (along_x[:, 3:-1] + along_x[:, 1:-3])
    total = total - 1.0 / 12.0 * (along_x[:, 4:] + along_x[:, :-4])
    total = total + 4.0 / 3.0 * (along_y[:, :, 3:-1] + along_y[:, :, 1:-3])
    total = total - 1.0 / 12.0 * (along_y[:, :, 4:] + along_y[:, :, :-4])
    return shifted - 0.5 * total


def factor_kernel(gram_ref, factor_ref, inverse_ref):
    order = gram_ref.shape[0]
    groups = order // 8
    sub = lax.broadcasted_iota(jnp.int32, (8, order), 0)
    lane = lax.broadcasted_iota(jnp.int32, (8, order), 1)
    gram = gram_ref[...]
    sym = 0.5 * (gram + gram.T)
    left = [sym[8 * i:8 * i + 8, :] for i in range(groups)]
    right = [jnp.where(lane == sub + 8 * i, 1.0, 0.0) for i in range(groups)]
    for k in range(order):
        home, place = divmod(k, 8)
        row = left[home][place:place + 1, :]
        row_right = right[home][place:place + 1, :]
        inverse = 1.0 / row[:, k:k + 1]
        for j in range(home, groups):
            column = left[j][:, k:k + 1] * inverse
            if j == home:
                column = jnp.where(sub[:, :1] > place, column, 0.0)
            left[j] = left[j] - column * row
            right[j] = right[j] - column * row_right
    for i in range(groups):
        pivots = jnp.sum(jnp.where(lane == sub + 8 * i, left[i], 0.0), axis=1, keepdims=True)
        scale = 1.0 / jnp.sqrt(pivots)
        factor_ref[pl.ds(8 * i, 8), :] = jnp.where(lane >= sub + 8 * i, left[i] * scale, 0.0)
        inverse_ref[pl.ds(8 * i, 8), :] = right[i] * scale


def factor_and_inverse(gram):
    shape = jax.ShapeDtypeStruct(gram.shape, jnp.float32)
    return pl.pallas_call(
        factor_kernel,
        out_shape=(shape, shape),
        in_specs=[pl.BlockSpec(memory_space=pltpu.VMEM)],
        out_specs=(pl.BlockSpec(memory_space=pltpu.VMEM),) * 2,
    )(gram)


def ring_rounds(stride):
    def flip(i):
        return i ^ stride

    def mirror(i):
        return i + (3 - 2 * ((i // stride) % 4)) * stride

    return [flip, mirror]


def butterfly_sum(value, axis):
    count = lax.axis_size(axis)
    if count & (count - 1):
        return lax.psum(value, axis)
    if count == 32:
        rounds = [lambda i: i ^ 1] + ring_rounds(2) + ring_rounds(8)
    elif count == 8:
        rounds = [lambda i: i ^ 1] + ring_rounds(2)
    else:
        rounds = [lambda i, mask=1 << b: i ^ mask for b in range(count.bit_length() - 1)]
    for partner in rounds:
        value = value + lax.ppermute(value, axis, [(i, partner(i)) for i in range(count)])
    return value


def shards(orbitals, potential):
    orbitals_here = lax.optimization_barrier(orbitals)
    first = apply_ham(orbitals_here, potential, orbitals) / 4.5
    filtered = 2.0 * apply_ham(first, potential) / 4.5 - orbitals_here
    count = filtered.shape[1] * filtered.shape[2] * filtered.shape[3]
    cells = count * lax.axis_size("gx") * lax.axis_size("gy")
    local_gram = (
        jnp.einsum(
            "kxyz,mxyz->km", filtered, filtered,
            precision=lax.Precision.HIGHEST, preferred_element_type=jnp.float32,
        )
        / cells
    )
    packed = local_gram.reshape(-1, 128)
    gram = butterfly_sum(butterfly_sum(packed, "gy"), "gx").reshape(local_gram.shape)
    factor, lower_inverse = factor_and_inverse(gram)
    basis = jnp.einsum(
        "mk,kxyz->mxyz", lower_inverse * jnp.sqrt(jnp.float32(cells)), filtered,
        precision=lax.Precision.HIGHEST, preferred_element_type=jnp.float32,
    )
    return (basis, factor)


def solution(mesh):
    return jax.shard_map(
        shards,
        mesh=mesh,
        in_specs=(P(None, "gx", "gy", None), P("gx", "gy", None)),
        out_specs=(P(None, "gx", "gy", None), P()),
        check_vma=False,
    )
```

```python
import jax
import jax.numpy as jnp
from jax import lax
from jax.experimental import pallas as pl
from jax.experimental.pallas import tpu as pltpu
from jax.sharding import PartitionSpec as P


def faces(cells, axis, dim, width):
    count = lax.axis_size(axis)
    size = cells.shape[dim]
    head = lax.slice_in_dim(cells, 0, width, axis=dim)
    tail = lax.slice_in_dim(cells, size - width, size, axis=dim)
    before = lax.ppermute(tail, axis, [(i, (i + 1) % count) for i in range(count)])
    after = lax.ppermute(head, axis, [((i + 1) % count, i) for i in range(count)])
    return jnp.concatenate([before, cells, after], axis=dim)


def apply_ham(core, pot, source=None):
    source = core if source is None else source
    along_x = faces(source, "gx", 1, 2)
    along_y = faces(source, "gy", 2, 2)
    if source is not core:
        along_x = jnp.concatenate([along_x[:, :2], core, along_x[:, -2:]], axis=1)
        along_y = jnp.concatenate([along_y[:, :, :2], core, along_y[:, :, -2:]], axis=2)
    size = core.shape[3]
    along_z = jnp.concatenate([core[..., size - 2:], core, core[..., :2]], axis=3)
    local = 4.0 / 3.0 * (along_z[..., 1:size + 1] + along_z[..., 3:size + 3])
    local = local - 1.0 / 12.0 * (along_z[..., :size] + along_z[..., 4:])
    total = lax.optimization_barrier(local) - 7.5 * core
    total = total + 4.0 / 3.0 * (along_x[:, 3:-1] + along_x[:, 1:-3])
    total = total - 1.0 / 12.0 * (along_x[:, 4:] + along_x[:, :-4])
    total = total + 4.0 / 3.0 * (along_y[:, :, 3:-1] + along_y[:, :, 1:-3])
    total = total - 1.0 / 12.0 * (along_y[:, :, 4:] + along_y[:, :, :-4])
    return -0.5 * total + pot[None] * core


def factor_kernel(gram_ref, factor_ref, inverse_ref):
    order = gram_ref.shape[0]
    groups = order // 8
    sub = lax.broadcasted_iota(jnp.int32, (8, order), 0)
    lane = lax.broadcasted_iota(jnp.int32, (8, order), 1)
    gram = gram_ref[...]
    sym = 0.5 * (gram + gram.T)
    left = [sym[8 * i:8 * i + 8, :] for i in range(groups)]
    right = [jnp.where(lane == sub + 8 * i, 1.0, 0.0) for i in range(groups)]
    for k in range(order):
        home, place = divmod(k, 8)
        row = left[home][place:place + 1, :]
        row_right = right[home][place:place + 1, :]
        inverse = 1.0 / row[:, k:k + 1]
        for j in range(home, groups):
            column = left[j][:, k:k + 1] * inverse
            if j == home:
                column = jnp.where(sub[:, :1] > place, column, 0.0)
            left[j] = left[j] - column * row
            right[j] = right[j] - column * row_right
    for i in range(groups):
        pivots = jnp.sum(jnp.where(lane == sub + 8 * i, left[i], 0.0), axis=1, keepdims=True)
        scale = 1.0 / jnp.sqrt(pivots)
        factor_ref[pl.ds(8 * i, 8), :] = jnp.where(lane >= sub + 8 * i, left[i] * scale, 0.0)
        inverse_ref[pl.ds(8 * i, 8), :] = right[i] * scale


def factor_and_inverse(gram):
    shape = jax.ShapeDtypeStruct(gram.shape, jnp.float32)
    return pl.pallas_call(
        factor_kernel,
        out_shape=(shape, shape),
        in_specs=[pl.BlockSpec(memory_space=pltpu.VMEM)],
        out_specs=(pl.BlockSpec(memory_space=pltpu.VMEM),) * 2,
    )(gram)


def ring_rounds(stride):
    def flip(i):
        return i ^ stride

    def mirror(i):
        return i + (3 - 2 * ((i // stride) % 4)) * stride

    return [flip, mirror]


def butterfly_sum(value, axis):
    count = lax.axis_size(axis)
    if count & (count - 1):
        return lax.psum(value, axis)
    if count == 32:
        rounds = [lambda i: i ^ 1] + ring_rounds(2) + ring_rounds(8)
    elif count == 8:
        rounds = [lambda i: i ^ 1] + ring_rounds(2)
    else:
        rounds = [lambda i, mask=1 << b: i ^ mask for b in range(count.bit_length() - 1)]
    for partner in rounds:
        value = value + lax.ppermute(value, axis, [(i, partner(i)) for i in range(count)])
    return value


def shards(orbitals, potential):
    orbitals_here = lax.optimization_barrier(orbitals)
    first = (apply_ham(orbitals_here, potential, orbitals) - 5.5 * orbitals_here) / 4.5
    applied = apply_ham(first, potential)
    filtered = 2.0 * (applied - 5.5 * first) / 4.5 - orbitals_here
    count = filtered.shape[1] * filtered.shape[2] * filtered.shape[3]
    cells = count * lax.axis_size("gx") * lax.axis_size("gy")
    local_gram = (
        jnp.einsum(
            "kxyz,mxyz->km", filtered, filtered,
            precision=lax.Precision.HIGHEST, preferred_element_type=jnp.float32,
        )
        / cells
    )
    packed = local_gram.reshape(-1, 128)
    gram = butterfly_sum(butterfly_sum(packed, "gy"), "gx").reshape(local_gram.shape)
    factor, lower_inverse = factor_and_inverse(gram)
    basis = jnp.einsum(
        "mk,kxyz->mxyz", lower_inverse * jnp.sqrt(jnp.float32(cells)), filtered,
        precision=lax.Precision.HIGHEST, preferred_element_type=jnp.float32,
    )
    return (basis, factor)


def solution(mesh):
    return jax.shard_map(
        shards,
        mesh=mesh,
        in_specs=(P(None, "gx", "gy", None), P("gx", "gy", None)),
        out_specs=(P(None, "gx", "gy", None), P()),
        check_vma=False,
    )
```
